256 devices in a mesh: gy: 32 (over y_lo, z, core), gz: 8 (over y_hi, x).
Axes of the slice: x: 4, y: 4 (y_hi: 2, y_lo: 2; y = y_hi * 2 + y_lo), z: 8, core: 2. Of those that a mesh axis runs over, the one named last changes fastest.
Arguments:
- field: float32 [1536, 512, 512], P('gy', 'gz'), may hold values from -4 to 4
Outputs:
- stepped: float32 [1536, 512, 512], P(('gy', 'gz'))
The draws below stay inside these ranges and needn't reach their ends.
All inputs are finite; a program needn't handle non-finite values.
Results may differ from the reference program's by a relative error of at most 0.0007.
Values sent between devices are 32-bit elements; how exact they have to be, the bound alone decides.
No kernel may reach another device: no remote copies, remote signals or barrier semaphores. Data moves between devices by JAX's collectives and lax.ppermute only.
A program may use at most 64 MiB of HBM per device.

```python
import jax
import jax.numpy as jnp
from jax import lax

NX = 512
LAMBDA = 9216
NY = 1536
NZ = 512


def draw_field(key, part):
    shape = (NY, NZ, NX)
    return jax.random.truncated_normal(key, -4.0, 4.0, shape, jnp.float32)


def setup_inputs(seed: int = 0) -> dict:
    arg_keys = jax.random.split(jax.random.key(seed), 2)
    field = draw_field(jax.random.fold_in(arg_keys[1], 71), 0)
    return {"field": field}


def explicit_axis(values, diffusion):
    zeros_rim = jnp.zeros_like(values[:1])
    before = jnp.concatenate([zeros_rim, values[:-1]], 0)
    behind = jnp.concatenate([values[1:], zeros_rim], 0)
    return (1.0 - 2.4 * diffusion) * values + (0.1 + 1.2 * diffusion) * (before + behind)

def implicit_axis(rhs_vals, diffusion):
    length = rhs_vals.shape[0]
    position = jnp.arange(length, dtype=jnp.int32)
    diagonal = jnp.full((length,), 1.0 + 2.4 * diffusion, rhs_vals.dtype)
    lower_band = jnp.where(position == 0, 0.0, 0.1 - 1.2 * diffusion).astype(rhs_vals.dtype)
    upper_band = jnp.where(position == length - 1, 0.0, 0.1 - 1.2 * diffusion).astype(rhs_vals.dtype)
    return lax.linalg.tridiagonal_solve(lower_band, diagonal, upper_band, rhs_vals)

def crank_axis(values, diffusion):
    return implicit_axis(explicit_axis(values, diffusion), diffusion)

def reference(field):
    diffusion = float(LAMBDA)

    def plane_step(plane_index):
        plane_vals = lax.dynamic_index_in_dim(field, plane_index, axis=1, keepdims=False)
        along_x = crank_axis(plane_vals.T, diffusion)
        return crank_axis(along_x.T, diffusion)
    planes = lax.map(plane_step, jnp.arange(NZ, dtype=jnp.int32))

    def row_step(row_index):
        row_vals = lax.dynamic_index_in_dim(planes, row_index, axis=1, keepdims=False)
        return crank_axis(row_vals, diffusion)
    return lax.map(row_step, jnp.arange(NY, dtype=jnp.int32))
```

```python
import math

import jax
import jax.numpy as jnp
from jax import lax
from jax.sharding import PartitionSpec as P

BLK = 128
LAMBDA = 9216


HIGHEST = lax.Precision.HIGHEST


def padded_2(cells, sides, width):
    for axis, dim in sides:
        count = lax.axis_size(axis)
        ends = count - 1
        head = lax.slice_in_dim(cells, 0, width, axis=dim)
        tail = lax.slice_in_dim(cells, cells.shape[dim] - width, cells.shape[dim], axis=dim)
        cells = jnp.concatenate(
            [
                lax.ppermute(tail, axis, [(i, (i + 1) % count) for i in range(ends)]),
                cells,
                lax.ppermute(head, axis, [((i + 1) % count, i) for i in range(ends)]),
            ],
            axis=dim,
        )
    return cells


def decay_constants(diffusion, length):
    diagonal = 1.0 + 2.4 * diffusion
    off_diag = 0.1 - 1.2 * diffusion
    big_root = 0.5 * (diagonal + math.sqrt(diagonal * diagonal - 4.0 * off_diag * off_diag))
    decay_ratio = -off_diag / big_root
    log_decay = math.log(decay_ratio)
    scaling = 1.0 / (
        big_root
        * (1.0 - decay_ratio * decay_ratio)
        * (1.0 - math.exp(2.0 * log_decay * (length + 1)))
    )
    return (log_decay, scaling)


def green_table(row_pos, col_pos, length, diffusion):
    log_decay, scaling = decay_constants(diffusion, length)
    nearer = jnp.minimum(row_pos, col_pos)
    farther = jnp.maximum(row_pos, col_pos)
    return (
        scaling
        * jnp.exp((farther - nearer) * log_decay)
        * -jnp.expm1((nearer + 1.0) * (2.0 * log_decay))
        * -jnp.expm1((length - farther) * (2.0 * log_decay))
    )


def explicit_local(values, line_dim, diffusion):
    length = values.shape[line_dim]
    zeros_rim = jnp.zeros_like(lax.slice_in_dim(values, 0, 1, axis=line_dim))
    before = jnp.concatenate(
        [zeros_rim, lax.slice_in_dim(values, 0, length - 1, axis=line_dim)], axis=line_dim
    )
    behind = jnp.concatenate(
        [lax.slice_in_dim(values, 1, length, axis=line_dim), zeros_rim], axis=line_dim
    )
    return (1.0 - 2.4 * diffusion) * values + (0.1 + 1.2 * diffusion) * (before + behind)


def line_solve(values, line_dim, diffusion, block_len):
    length = values.shape[line_dim]
    pieces = length // block_len
    couple = 1.2 * diffusion - 0.1
    within = jnp.arange(block_len, dtype=jnp.float32)
    local_inverse = green_table(within[:, None], within[None, :], block_len, diffusion)
    piece_pos = jnp.arange(pieces, dtype=jnp.float32)
    side_pos = jnp.arange(2, dtype=jnp.float32)
    row_pos = piece_pos[:, None, None, None] * block_len + within[None, :, None, None]
    col_pos = (
        piece_pos[None, None, :, None] * block_len
        - 1.0
        + side_pos[None, None, None, :] * (block_len + 1.0)
    )
    coupling = couple * green_table(row_pos, col_pos, length, diffusion)
    if line_dim == 2:
        lead_len, tail_len = (values.shape[0], values.shape[1])
        splitted = values.reshape(lead_len, tail_len, pieces, block_len)
        solved = jnp.einsum("abqj,ij->abqi", splitted, local_inverse, precision=HIGHEST)
        rim_values = jnp.stack([solved[..., 0], solved[..., block_len - 1]], axis=-1)
        corrected = solved + jnp.einsum("abks,qiks->abqi", rim_values, coupling, precision=HIGHEST)
        return corrected.reshape(lead_len, tail_len, length)
    lead_len, tail_len = (values.shape[0], values.shape[2])
    splitted = values.reshape(lead_len, pieces, block_len, tail_len)
    solved = jnp.einsum("aqjb,ij->aqib", splitted, local_inverse, precision=HIGHEST)
    rim_values = jnp.stack([solved[:, :, 0, :], solved[:, :, block_len - 1, :]], axis=2)
    corrected = solved + jnp.einsum("aksb,qiks->aqib", rim_values, coupling, precision=HIGHEST)
    return corrected.reshape(lead_len, length, tail_len)


def shifted(values, axis, step):
    count = lax.axis_size(axis)
    if step > 0:
        pairs = [(i, i + step) for i in range(count - step)]
    else:
        pairs = [(i - step, i) for i in range(count + step)]
    return lax.ppermute(values, axis, pairs)


def decayed_scan(values, axis, step_sign, ratio):
    count = lax.axis_size(axis)
    total = values
    span = 1
    while span < count:
        total = total + (ratio ** span) * shifted(total, axis, step_sign * span)
        span *= 2
    return total


def y_solve(along_x, head, tail, diffusion):
    y_rows = along_x.shape[0]
    before = lax.ppermute(tail, "gy", [(i, i + 1) for i in range(lax.axis_size("gy") - 1)])
    behind = lax.ppermute(head, "gy", [(i + 1, i) for i in range(lax.axis_size("gy") - 1)])
    padded = jnp.concatenate([before, along_x, behind], axis=0)
    rhs_y = (1.0 - 2.4 * diffusion) * along_x + (0.1 + 1.2 * diffusion) * (padded[:-2] + padded[2:])
    within = jnp.arange(y_rows, dtype=jnp.float32)
    local_inverse = green_table(within[:, None], within[None, :], y_rows, diffusion)
    rim_inverse = jnp.stack([local_inverse[0], local_inverse[y_rows - 1]])
    rims = jnp.einsum("ij,jzx->izx", rim_inverse, rhs_y, precision=HIGHEST)
    solved = jnp.einsum("ij,jzx->izx", local_inverse, rhs_y, precision=HIGHEST)
    first, last = rims[0], rims[1]

    devices = lax.axis_size("gy")
    length = devices * y_rows
    log_decay, scaling = decay_constants(diffusion, length)
    ratio = math.exp(log_decay)
    block_ratio = math.exp(log_decay * y_rows)
    couple = 1.2 * diffusion - 0.1
    start = lax.axis_index("gy").astype(jnp.float32) * y_rows

    def one_minus(power):
        return -jnp.expm1(power * (2.0 * log_decay))

    lead_first = one_minus(start)
    tail_last = one_minus(length - start - y_rows)
    left_part = ratio ** (y_rows + 1) * lead_first * first + one_minus(start + y_rows + 1) * last
    right_part = one_minus(length - start + 1) * first + ratio ** (y_rows + 1) * tail_last * last
    left_scan = decayed_scan(left_part, "gy", 1, block_ratio)
    right_scan = decayed_scan(right_part, "gy", -1, block_ratio)
    left_sum = (left_scan - left_part) / block_ratio + ratio * lead_first * first
    right_sum = (right_scan - right_part) / block_ratio + ratio * tail_last * last

    row_pos = start + within
    left_gain = (couple * scaling) * one_minus(length - row_pos) * jnp.exp(within * log_decay)
    right_gain = (couple * scaling) * one_minus(row_pos + 1.0) * jnp.exp((y_rows - 1.0 - within) * log_decay)
    return solved + left_gain[:, None, None] * left_sum[None] + right_gain[:, None, None] * right_sum[None]


def per_device(field):
    diffusion = float(LAMBDA)
    y_rows = field.shape[0]
    edges = jnp.stack([field[0], field[y_rows - 1]])
    edge_x = line_solve(explicit_local(edges, 2, diffusion), 2, diffusion, BLK)
    along_x = line_solve(explicit_local(field, 2, diffusion), 2, diffusion, BLK)
    along_y = y_solve(along_x, edge_x[0:1], edge_x[1:2], diffusion)
    pencils = lax.all_to_all(along_y, "gz", split_axis=0, concat_axis=1, tiled=True)
    return line_solve(explicit_local(pencils, 1, diffusion), 1, diffusion, BLK)


def solution(mesh):
    placed = (P("gy", "gz", None),)
    return jax.shard_map(
        per_device,
        mesh=mesh,
        in_specs=placed,
        out_specs=P(("gy", "gz"), None, None),
        check_vma=False,
    )
```

```python
import math

import jax
import jax.numpy as jnp
from jax import lax
from jax.sharding import PartitionSpec as P

BLK = 128
LAMBDA = 9216


HIGHEST = lax.Precision.HIGHEST


def padded_2(cells, sides, width):
    for axis, dim in sides:
        count = lax.axis_size(axis)
        ends = count - 1
        head = lax.slice_in_dim(cells, 0, width, axis=dim)
        tail = lax.slice_in_dim(cells, cells.shape[dim] - width, cells.shape[dim], axis=dim)
        cells = jnp.concatenate(
            [
                lax.ppermute(tail, axis, [(i, (i + 1) % count) for i in range(ends)]),
                cells,
                lax.ppermute(head, axis, [((i + 1) % count, i) for i in range(ends)]),
            ],
            axis=dim,
        )
    return cells


def decay_constants(diffusion, length):
    diagonal = 1.0 + 2.4 * diffusion
    off_diag = 0.1 - 1.2 * diffusion
    big_root = 0.5 * (diagonal + math.sqrt(diagonal * diagonal - 4.0 * off_diag * off_diag))
    decay_ratio = -off_diag / big_root
    log_decay = math.log(decay_ratio)
    scaling = 1.0 / (
        big_root
        * (1.0 - decay_ratio * decay_ratio)
        * (1.0 - math.exp(2.0 * log_decay * (length + 1)))
    )
    return (log_decay, scaling)


def green_table(row_pos, col_pos, length, diffusion):
    log_decay, scaling = decay_constants(diffusion, length)
    nearer = jnp.minimum(row_pos, col_pos)
    farther = jnp.maximum(row_pos, col_pos)
    return (
        scaling
        * jnp.exp((farther - nearer) * log_decay)
        * -jnp.expm1((nearer + 1.0) * (2.0 * log_decay))
        * -jnp.expm1((length - farther) * (2.0 * log_decay))
    )


def explicit_local(values, line_dim, diffusion):
    length = values.shape[line_dim]
    zeros_rim = jnp.zeros_like(lax.slice_in_dim(values, 0, 1, axis=line_dim))
    before = jnp.concatenate(
        [zeros_rim, lax.slice_in_dim(values, 0, length - 1, axis=line_dim)], axis=line_dim
    )
    behind = jnp.concatenate(
        [lax.slice_in_dim(values, 1, length, axis=line_dim), zeros_rim], axis=line_dim
    )
    return (1.0 - 2.4 * diffusion) * values + (0.1 + 1.2 * diffusion) * (before + behind)


def line_solve(values, line_dim, diffusion, block_len):
    length = values.shape[line_dim]
    pieces = length // block_len
    couple = 1.2 * diffusion - 0.1
    within = jnp.arange(block_len, dtype=jnp.float32)
    local_inverse = green_table(within[:, None], within[None, :], block_len, diffusion)
    piece_pos = jnp.arange(pieces, dtype=jnp.float32)
    side_pos = jnp.arange(2, dtype=jnp.float32)
    row_pos = piece_pos[:, None, None, None] * block_len + within[None, :, None, None]
    col_pos = (
        piece_pos[None, None, :, None] * block_len
        - 1.0
        + side_pos[None, None, None, :] * (block_len + 1.0)
    )
    coupling = couple * green_table(row_pos, col_pos, length, diffusion)
    if line_dim == 2:
        lead_len, tail_len = (values.shape[0], values.shape[1])
        splitted = values.reshape(lead_len, tail_len, pieces, block_len)
        solved = jnp.einsum("abqj,ij->abqi", splitted, local_inverse, precision=HIGHEST)
        rim_values = jnp.stack([solved[..., 0], solved[..., block_len - 1]], axis=-1)
        corrected = solved + jnp.einsum("abks,qiks->abqi", rim_values, coupling, precision=HIGHEST)
        return corrected.reshape(lead_len, tail_len, length)
    lead_len, tail_len = (values.shape[0], values.shape[2])
    splitted = values.reshape(lead_len, pieces, block_len, tail_len)
    solved = jnp.einsum("aqjb,ij->aqib", splitted, local_inverse, precision=HIGHEST)
    rim_values = jnp.stack([solved[:, :, 0, :], solved[:, :, block_len - 1, :]], axis=2)
    corrected = solved + jnp.einsum("aksb,qiks->aqib", rim_values, coupling, precision=HIGHEST)
    return corrected.reshape(lead_len, length, tail_len)


def shifted(values, axis, step):
    count = lax.axis_size(axis)
    if step > 0:
        pairs = [(i, i + step) for i in range(count - step)]
    else:
        pairs = [(i - step, i) for i in range(count + step)]
    return lax.ppermute(values, axis, pairs)


def decayed_scan(values, axis, step_sign, ratio):
    count = lax.axis_size(axis)
    total = values
    span = 1
    while span < count:
        total = total + (ratio ** span) * shifted(total, axis, step_sign * span)
        span *= 2
    return total


def y_solve(along_x, head, tail, diffusion):
    y_rows = along_x.shape[0]
    before = lax.ppermute(tail, "gy", [(i, i + 1) for i in range(lax.axis_size("gy") - 1)])
    behind = lax.ppermute(head, "gy", [(i + 1, i) for i in range(lax.axis_size("gy") - 1)])
    padded = jnp.concatenate([before, along_x, behind], axis=0)
    rhs_y = (1.0 - 2.4 * diffusion) * along_x + (0.1 + 1.2 * diffusion) * (padded[:-2] + padded[2:])
    within = jnp.arange(y_rows, dtype=jnp.float32)
    local_inverse = green_table(within[:, None], within[None, :], y_rows, diffusion)
    rim_inverse = jnp.stack([local_inverse[0], local_inverse[y_rows - 1]])
    rims = jnp.einsum("ij,jzx->izx", rim_inverse, rhs_y, precision=HIGHEST)
    solved = lax.optimization_barrier(
        jnp.einsum("ij,jzx->izx", local_inverse, rhs_y, precision=HIGHEST)
    )
    first, last = rims[0], rims[1]

    devices = lax.axis_size("gy")
    length = devices * y_rows
    log_decay, scaling = decay_constants(diffusion, length)
    ratio = math.exp(log_decay)
    block_ratio = math.exp(log_decay * y_rows)
    couple = 1.2 * diffusion - 0.1
    start = lax.axis_index("gy").astype(jnp.float32) * y_rows

    def one_minus(power):
        return -jnp.expm1(power * (2.0 * log_decay))

    lead_first = one_minus(start)
    tail_last = one_minus(length - start - y_rows)
    left_part = ratio ** (y_rows + 1) * lead_first * first + one_minus(start + y_rows + 1) * last
    right_part = one_minus(length - start + 1) * first + ratio ** (y_rows + 1) * tail_last * last
    left_scan = decayed_scan(left_part, "gy", 1, block_ratio)
    right_scan = decayed_scan(right_part, "gy", -1, block_ratio)
    left_sum = (left_scan - left_part) / block_ratio + ratio * lead_first * first
    right_sum = (right_scan - right_part) / block_ratio + ratio * tail_last * last

    row_pos = start + within
    left_gain = (couple * scaling) * one_minus(length - row_pos) * jnp.exp(within * log_decay)
    right_gain = (couple * scaling) * one_minus(row_pos + 1.0) * jnp.exp((y_rows - 1.0 - within) * log_decay)
    return solved + left_gain[:, None, None] * left_sum[None] + right_gain[:, None, None] * right_sum[None]


def explicit_full(values, line_dim, diffusion):
    width = [(0, 0)] * values.ndim
    width[line_dim] = (1, 1)
    padded = jnp.pad(values, width)
    length = values.shape[line_dim]
    before = lax.slice_in_dim(padded, 0, length, axis=line_dim)
    behind = lax.slice_in_dim(padded, 2, length + 2, axis=line_dim)
    return (1.0 - 2.4 * diffusion) * values + (0.1 + 1.2 * diffusion) * (before + behind)


def full_inverse(length, diffusion):
    pos = jnp.arange(length, dtype=jnp.float32)
    return green_table(pos[:, None], pos[None, :], length, diffusion)


def x_solve(values, diffusion):
    inverse = full_inverse(values.shape[2], diffusion)
    return jnp.einsum("azj,ij->azi", explicit_full(values, 2, diffusion), inverse, precision=HIGHEST)


def z_solve(values, diffusion):
    inverse = full_inverse(values.shape[1], diffusion)
    return jnp.einsum("ij,ajx->aix", inverse, explicit_full(values, 1, diffusion), precision=HIGHEST)


CHUNKS = 2


def per_device(field):
    diffusion = float(LAMBDA)
    y_rows = field.shape[0]
    edges = jnp.stack([field[0], field[y_rows - 1]])
    edge_x = x_solve(edges, diffusion)
    along_x = x_solve(field, diffusion)
    along_y = y_solve(along_x, edge_x[0:1], edge_x[1:2], diffusion)
    width = along_y.shape[2] // CHUNKS
    parts = []
    for k in range(CHUNKS):
        piece = along_y[:, :, k * width:(k + 1) * width]
        pencils = lax.all_to_all(piece, "gz", split_axis=0, concat_axis=1, tiled=True)
        parts.append(z_solve(pencils, diffusion))
    return jnp.concatenate(parts, axis=2)


def solution(mesh):
    placed = (P("gy", "gz", None),)
    return jax.shard_map(
        per_device,
        mesh=mesh,
        in_specs=placed,
        out_specs=P(("gy", "gz"), None, None),
        check_vma=False,
    )
```

```python
import math

import jax
import jax.numpy as jnp
from jax import lax
from jax.sharding import PartitionSpec as P

BLK = 128
LAMBDA = 9216


HIGHEST = lax.Precision.HIGHEST


def padded_2(cells, sides, width):
    for axis, dim in sides:
        count = lax.axis_size(axis)
        ends = count - 1
        head = lax.slice_in_dim(cells, 0, width, axis=dim)
        tail = lax.slice_in_dim(cells, cells.shape[dim] - width, cells.shape[dim], axis=dim)
        cells = jnp.concatenate(
            [
                lax.ppermute(tail, axis, [(i, (i + 1) % count) for i in range(ends)]),
                cells,
                lax.ppermute(head, axis, [((i + 1) % count, i) for i in range(ends)]),
            ],
            axis=dim,
        )
    return cells


def decay_constants(diffusion, length):
    diagonal = 1.0 + 2.4 * diffusion
    off_diag = 0.1 - 1.2 * diffusion
    big_root = 0.5 * (diagonal + math.sqrt(diagonal * diagonal - 4.0 * off_diag * off_diag))
    decay_ratio = -off_diag / big_root
    log_decay = math.log(decay_ratio)
    scaling = 1.0 / (
        big_root
        * (1.0 - decay_ratio * decay_ratio)
        * (1.0 - math.exp(2.0 * log_decay * (length + 1)))
    )
    return (log_decay, scaling)


def green_table(row_pos, col_pos, length, diffusion):
    log_decay, scaling = decay_constants(diffusion, length)
    nearer = jnp.minimum(row_pos, col_pos)
    farther = jnp.maximum(row_pos, col_pos)
    return (
        scaling
        * jnp.exp((farther - nearer) * log_decay)
        * -jnp.expm1((nearer + 1.0) * (2.0 * log_decay))
        * -jnp.expm1((length - farther) * (2.0 * log_decay))
    )


def explicit_local(values, line_dim, diffusion):
    length = values.shape[line_dim]
    zeros_rim = jnp.zeros_like(lax.slice_in_dim(values, 0, 1, axis=line_dim))
    before = jnp.concatenate(
        [zeros_rim, lax.slice_in_dim(values, 0, length - 1, axis=line_dim)], axis=line_dim
    )
    behind = jnp.concatenate(
        [lax.slice_in_dim(values, 1, length, axis=line_dim), zeros_rim], axis=line_dim
    )
    return (1.0 - 2.4 * diffusion) * values + (0.1 + 1.2 * diffusion) * (before + behind)


def line_solve(values, line_dim, diffusion, block_len):
    length = values.shape[line_dim]
    pieces = length // block_len
    couple = 1.2 * diffusion - 0.1
    within = jnp.arange(block_len, dtype=jnp.float32)
    local_inverse = green_table(within[:, None], within[None, :], block_len, diffusion)
    piece_pos = jnp.arange(pieces, dtype=jnp.float32)
    side_pos = jnp.arange(2, dtype=jnp.float32)
    row_pos = piece_pos[:, None, None, None] * block_len + within[None, :, None, None]
    col_pos = (
        piece_pos[None, None, :, None] * block_len
        - 1.0
        + side_pos[None, None, None, :] * (block_len + 1.0)
    )
    coupling = couple * green_table(row_pos, col_pos, length, diffusion)
    if line_dim == 2:
        lead_len, tail_len = (values.shape[0], values.shape[1])
        splitted = values.reshape(lead_len, tail_len, pieces, block_len)
        solved = jnp.einsum("abqj,ij->abqi", splitted, local_inverse, precision=HIGHEST)
        rim_values = jnp.stack([solved[..., 0], solved[..., block_len - 1]], axis=-1)
        corrected = solved + jnp.einsum("abks,qiks->abqi", rim_values, coupling, precision=HIGHEST)
        return corrected.reshape(lead_len, tail_len, length)
    lead_len, tail_len = (values.shape[0], values.shape[2])
    splitted = values.reshape(lead_len, pieces, block_len, tail_len)
    solved = jnp.einsum("aqjb,ij->aqib", splitted, local_inverse, precision=HIGHEST)
    rim_values = jnp.stack([solved[:, :, 0, :], solved[:, :, block_len - 1, :]], axis=2)
    corrected = solved + jnp.einsum("aksb,qiks->aqib", rim_values, coupling, precision=HIGHEST)
    return corrected.reshape(lead_len, length, tail_len)


def shifted(values, axis, step):
    count = lax.axis_size(axis)
    if step > 0:
        pairs = [(i, i + step) for i in range(count - step)]
    else:
        pairs = [(i - step, i) for i in range(count + step)]
    return lax.ppermute(values, axis, pairs)


RADIX = 4


def decayed_scan(values, axis, step_sign, ratio):
    count = lax.axis_size(axis)
    total = values
    span = 1
    while span < count:
        gathered = total
        for multiple in range(1, RADIX):
            step = multiple * span
            if step < count:
                gathered = gathered + (ratio ** step) * shifted(total, axis, step_sign * step)
        total = gathered
        span *= RADIX
    return total


def y_solve(along_x, head, tail, diffusion):
    y_rows = along_x.shape[0]
    before = lax.ppermute(tail, "gy", [(i, i + 1) for i in range(lax.axis_size("gy") - 1)])
    behind = lax.ppermute(head, "gy", [(i + 1, i) for i in range(lax.axis_size("gy") - 1)])
    padded = jnp.concatenate([before, along_x, behind], axis=0)
    rhs_y = (1.0 - 2.4 * diffusion) * along_x + (0.1 + 1.2 * diffusion) * (padded[:-2] + padded[2:])
    within = jnp.arange(y_rows, dtype=jnp.float32)
    local_inverse = green_table(within[:, None], within[None, :], y_rows, diffusion)
    rim_inverse = jnp.stack([local_inverse[0], local_inverse[y_rows - 1]])
    rims = jnp.einsum("ij,jzx->izx", rim_inverse, rhs_y, precision=HIGHEST)
    solved = lax.optimization_barrier(
        jnp.einsum("ij,jzx->izx", local_inverse, rhs_y, precision=HIGHEST)
    )
    first, last = rims[0], rims[1]

    devices = lax.axis_size("gy")
    length = devices * y_rows
    log_decay, scaling = decay_constants(diffusion, length)
    ratio = math.exp(log_decay)
    block_ratio = math.exp(log_decay * y_rows)
    couple = 1.2 * diffusion - 0.1
    start = lax.axis_index("gy").astype(jnp.float32) * y_rows

    def one_minus(power):
        return -jnp.expm1(power * (2.0 * log_decay))

    lead_first = one_minus(start)
    tail_last = one_minus(length - start - y_rows)
    left_part = ratio ** (y_rows + 1) * lead_first * first + one_minus(start + y_rows + 1) * last
    right_part = one_minus(length - start + 1) * first + ratio ** (y_rows + 1) * tail_last * last
    left_scan = decayed_scan(left_part, "gy", 1, block_ratio)
    right_scan = decayed_scan(right_part, "gy", -1, block_ratio)
    left_sum = (left_scan - left_part) / block_ratio + ratio * lead_first * first
    right_sum = (right_scan - right_part) / block_ratio + ratio * tail_last * last

    row_pos = start + within
    left_gain = (couple * scaling) * one_minus(length - row_pos) * jnp.exp(within * log_decay)
    right_gain = (couple * scaling) * one_minus(row_pos + 1.0) * jnp.exp((y_rows - 1.0 - within) * log_decay)
    return solved + left_gain[:, None, None] * left_sum[None] + right_gain[:, None, None] * right_sum[None]


def explicit_full(values, line_dim, diffusion):
    width = [(0, 0)] * values.ndim
    width[line_dim] = (1, 1)
    padded = jnp.pad(values, width)
    length = values.shape[line_dim]
    before = lax.slice_in_dim(padded, 0, length, axis=line_dim)
    behind = lax.slice_in_dim(padded, 2, length + 2, axis=line_dim)
    return (1.0 - 2.4 * diffusion) * values + (0.1 + 1.2 * diffusion) * (before + behind)


def full_inverse(length, diffusion):
    pos = jnp.arange(length, dtype=jnp.float32)
    return green_table(pos[:, None], pos[None, :], length, diffusion)


def x_solve(values, diffusion):
    inverse = full_inverse(values.shape[2], diffusion)
    return jnp.einsum("azj,ij->azi", explicit_full(values, 2, diffusion), inverse, precision=HIGHEST)


def z_solve(values, diffusion):
    inverse = full_inverse(values.shape[1], diffusion)
    return jnp.einsum("ij,ajx->aix", inverse, explicit_full(values, 1, diffusion), precision=HIGHEST)


CHUNKS = 2


def per_device(field):
    diffusion = float(LAMBDA)
    y_rows = field.shape[0]
    edges = jnp.stack([field[0], field[y_rows - 1]])
    edge_x = x_solve(edges, diffusion)
    along_x = x_solve(field, diffusion)
    along_y = y_solve(along_x, edge_x[0:1], edge_x[1:2], diffusion)
    width = along_y.shape[2] // CHUNKS
    parts = []
    for k in range(CHUNKS):
        piece = along_y[:, :, k * width:(k + 1) * width]
        pencils = lax.all_to_all(piece, "gz", split_axis=0, concat_axis=1, tiled=True)
        parts.append(z_solve(pencils, diffusion))
    return jnp.concatenate(parts, axis=2)


def solution(mesh):
    placed = (P("gy", "gz", None),)
    return jax.shard_map(
        per_device,
        mesh=mesh,
        in_specs=placed,
        out_specs=P(("gy", "gz"), None, None),
        check_vma=False,
    )
```

```python
import math

import jax
import jax.numpy as jnp
from jax import lax
from jax.sharding import PartitionSpec as P

BLK = 128
LAMBDA = 9216


HIGHEST = lax.Precision.HIGHEST


def padded_2(cells, sides, width):
    for axis, dim in sides:
        count = lax.axis_size(axis)
        ends = count - 1
        head = lax.slice_in_dim(cells, 0, width, axis=dim)
        tail = lax.slice_in_dim(cells, cells.shape[dim] - width, cells.shape[dim], axis=dim)
        cells = jnp.concatenate(
            [
                lax.ppermute(tail, axis, [(i, (i + 1) % count) for i in range(ends)]),
                cells,
                lax.ppermute(head, axis, [((i + 1) % count, i) for i in range(ends)]),
            ],
            axis=dim,
        )
    return cells


def decay_constants(diffusion, length):
    diagonal = 1.0 + 2.4 * diffusion
    off_diag = 0.1 - 1.2 * diffusion
    big_root = 0.5 * (diagonal + math.sqrt(diagonal * diagonal - 4.0 * off_diag * off_diag))
    decay_ratio = -off_diag / big_root
    log_decay = math.log(decay_ratio)
    scaling = 1.0 / (
        big_root
        * (1.0 - decay_ratio * decay_ratio)
        * (1.0 - math.exp(2.0 * log_decay * (length + 1)))
    )
    return (log_decay, scaling)


def green_table(row_pos, col_pos, length, diffusion):
    log_decay, scaling = decay_constants(diffusion, length)
    nearer = jnp.minimum(row_pos, col_pos)
    farther = jnp.maximum(row_pos, col_pos)
    return (
        scaling
        * jnp.exp((farther - nearer) * log_decay)
        * -jnp.expm1((nearer + 1.0) * (2.0 * log_decay))
        * -jnp.expm1((length - farther) * (2.0 * log_decay))
    )


def explicit_local(values, line_dim, diffusion):
    length = values.shape[line_dim]
    zeros_rim = jnp.zeros_like(lax.slice_in_dim(values, 0, 1, axis=line_dim))
    before = jnp.concatenate(
        [zeros_rim, lax.slice_in_dim(values, 0, length - 1, axis=line_dim)], axis=line_dim
    )
    behind = jnp.concatenate(
        [lax.slice_in_dim(values, 1, length, axis=line_dim), zeros_rim], axis=line_dim
    )
    return (1.0 - 2.4 * diffusion) * values + (0.1 + 1.2 * diffusion) * (before + behind)


def line_solve(values, line_dim, diffusion, block_len):
    length = values.shape[line_dim]
    pieces = length // block_len
    couple = 1.2 * diffusion - 0.1
    within = jnp.arange(block_len, dtype=jnp.float32)
    local_inverse = green_table(within[:, None], within[None, :], block_len, diffusion)
    piece_pos = jnp.arange(pieces, dtype=jnp.float32)
    side_pos = jnp.arange(2, dtype=jnp.float32)
    row_pos = piece_pos[:, None, None, None] * block_len + within[None, :, None, None]
    col_pos = (
        piece_pos[None, None, :, None] * block_len
        - 1.0
        + side_pos[None, None, None, :] * (block_len + 1.0)
    )
    coupling = couple * green_table(row_pos, col_pos, length, diffusion)
    if line_dim == 2:
        lead_len, tail_len = (values.shape[0], values.shape[1])
        splitted = values.reshape(lead_len, tail_len, pieces, block_len)
        solved = jnp.einsum("abqj,ij->abqi", splitted, local_inverse, precision=HIGHEST)
        rim_values = jnp.stack([solved[..., 0], solved[..., block_len - 1]], axis=-1)
        corrected = solved + jnp.einsum("abks,qiks->abqi", rim_values, coupling, precision=HIGHEST)
        return corrected.reshape(lead_len, tail_len, length)
    lead_len, tail_len = (values.shape[0], values.shape[2])
    splitted = values.reshape(lead_len, pieces, block_len, tail_len)
    solved = jnp.einsum("aqjb,ij->aqib", splitted, local_inverse, precision=HIGHEST)
    rim_values = jnp.stack([solved[:, :, 0, :], solved[:, :, block_len - 1, :]], axis=2)
    corrected = solved + jnp.einsum("aksb,qiks->aqib", rim_values, coupling, precision=HIGHEST)
    return corrected.reshape(lead_len, length, tail_len)


def shifted(values, axis, step):
    count = lax.axis_size(axis)
    if step > 0:
        pairs = [(i, i + step) for i in range(count - step)]
    else:
        pairs = [(i - step, i) for i in range(count + step)]
    return lax.ppermute(values, axis, pairs)


def butterfly_scans(left, right, axis, ratio):
    count = lax.axis_size(axis)
    assert count & (count - 1) == 0
    me = lax.axis_index(axis)
    left_total, right_total = left, right
    left_excl = jnp.zeros_like(left)
    right_excl = jnp.zeros_like(right)
    half = 1
    while half < count:
        pairs = [(i, i ^ half) for i in range(count)]
        got = lax.ppermute(jnp.stack([left_total, right_total]), axis, pairs)
        upper = (me & half) != 0
        base = me - (me % (2 * half))
        mid_gap = (me - base - half).astype(jnp.float32)
        low_gap = (base + half - 1 - me).astype(jnp.float32)
        left_gain = jnp.where(upper, jnp.exp(mid_gap * math.log(ratio)), 0.0)
        right_gain = jnp.where(upper, 0.0, jnp.exp(low_gap * math.log(ratio)))
        left_excl = left_excl + left_gain * got[0]
        right_excl = right_excl + right_gain * got[1]
        decay = ratio ** half
        left_total = jnp.where(upper, left_total + decay * got[0], decay * left_total + got[0])
        right_total = jnp.where(upper, got[1] + decay * right_total, right_total + decay * got[1])
        half *= 2
    return left_excl, right_excl


def y_solve(along_x, head, tail, diffusion):
    y_rows = along_x.shape[0]
    before = lax.ppermute(tail, "gy", [(i, i + 1) for i in range(lax.axis_size("gy") - 1)])
    behind = lax.ppermute(head, "gy", [(i + 1, i) for i in range(lax.axis_size("gy") - 1)])
    padded = jnp.concatenate([before, along_x, behind], axis=0)
    rhs_y = (1.0 - 2.4 * diffusion) * along_x + (0.1 + 1.2 * diffusion) * (padded[:-2] + padded[2:])
    within = jnp.arange(y_rows, dtype=jnp.float32)
    local_inverse = green_table(within[:, None], within[None, :], y_rows, diffusion)
    rim_inverse = jnp.stack([local_inverse[0], local_inverse[y_rows - 1]])
    rims = jnp.einsum("ij,jzx->izx", rim_inverse, rhs_y, precision=HIGHEST)
    solved = lax.optimization_barrier(
        jnp.einsum("ij,jzx->izx", local_inverse, rhs_y, precision=HIGHEST)
    )
    first, last = rims[0], rims[1]

    devices = lax.axis_size("gy")
    length = devices * y_rows
    log_decay, scaling = decay_constants(diffusion, length)
    ratio = math.exp(log_decay)
    block_ratio = math.exp(log_decay * y_rows)
    couple = 1.2 * diffusion - 0.1
    start = lax.axis_index("gy").astype(jnp.float32) * y_rows

    def one_minus(power):
        return -jnp.expm1(power * (2.0 * log_decay))

    lead_first = one_minus(start)
    tail_last = one_minus(length - start - y_rows)
    left_part = ratio ** (y_rows + 1) * lead_first * first + one_minus(start + y_rows + 1) * last
    right_part = one_minus(length - start + 1) * first + ratio ** (y_rows + 1) * tail_last * last
    left_excl, right_excl = butterfly_scans(left_part, right_part, "gy", block_ratio)
    left_sum = left_excl + ratio * lead_first * first
    right_sum = right_excl + ratio * tail_last * last

    row_pos = start + within
    left_gain = (couple * scaling) * one_minus(length - row_pos) * jnp.exp(within * log_decay)
    right_gain = (couple * scaling) * one_minus(row_pos + 1.0) * jnp.exp((y_rows - 1.0 - within) * log_decay)
    return solved + left_gain[:, None, None] * left_sum[None] + right_gain[:, None, None] * right_sum[None]


def explicit_full(values, line_dim, diffusion):
    width = [(0, 0)] * values.ndim
    width[line_dim] = (1, 1)
    padded = jnp.pad(values, width)
    length = values.shape[line_dim]
    before = lax.slice_in_dim(padded, 0, length, axis=line_dim)
    behind = lax.slice_in_dim(padded, 2, length + 2, axis=line_dim)
    return (1.0 - 2.4 * diffusion) * values + (0.1 + 1.2 * diffusion) * (before + behind)


def full_inverse(length, diffusion):
    pos = jnp.arange(length, dtype=jnp.float32)
    return green_table(pos[:, None], pos[None, :], length, diffusion)


def x_solve(values, diffusion):
    inverse = full_inverse(values.shape[2], diffusion)
    return jnp.einsum("azj,ij->azi", explicit_full(values, 2, diffusion), inverse, precision=HIGHEST)


def z_solve(values, diffusion):
    inverse = full_inverse(values.shape[1], diffusion)
    return jnp.einsum("ij,ajx->aix", inverse, explicit_full(values, 1, diffusion), precision=HIGHEST)


CHUNKS = 2


def per_device(field):
    diffusion = float(LAMBDA)
    y_rows = field.shape[0]
    edges = jnp.stack([field[0], field[y_rows - 1]])
    edge_x = x_solve(edges, diffusion)
    along_x = x_solve(field, diffusion)
    along_y = y_solve(along_x, edge_x[0:1], edge_x[1:2], diffusion)
    width = along_y.shape[2] // CHUNKS
    parts = []
    for k in range(CHUNKS):
        piece = along_y[:, :, k * width:(k + 1) * width]
        pencils = lax.all_to_all(piece, "gz", split_axis=0, concat_axis=1, tiled=True)
        parts.append(z_solve(pencils, diffusion))
    return jnp.concatenate(parts, axis=2)


def solution(mesh):
    placed = (P("gy", "gz", None),)
    return jax.shard_map(
        per_device,
        mesh=mesh,
        in_specs=placed,
        out_specs=P(("gy", "gz"), None, None),
        check_vma=False,
    )
```

```python
import math

import jax
import jax.numpy as jnp
from jax import lax
from jax.sharding import PartitionSpec as P

BLK = 128
LAMBDA = 9216


HIGHEST = lax.Precision.HIGHEST


def padded_2(cells, sides, width):
    for axis, dim in sides:
        count = lax.axis_size(axis)
        ends = count - 1
        head = lax.slice_in_dim(cells, 0, width, axis=dim)
        tail = lax.slice_in_dim(cells, cells.shape[dim] - width, cells.shape[dim], axis=dim)
        cells = jnp.concatenate(
            [
                lax.ppermute(tail, axis, [(i, (i + 1) % count) for i in range(ends)]),
                cells,
                lax.ppermute(head, axis, [((i + 1) % count, i) for i in range(ends)]),
            ],
            axis=dim,
        )
    return cells


def decay_constants(diffusion, length):
    diagonal = 1.0 + 2.4 * diffusion
    off_diag = 0.1 - 1.2 * diffusion
    big_root = 0.5 * (diagonal + math.sqrt(diagonal * diagonal - 4.0 * off_diag * off_diag))
    decay_ratio = -off_diag / big_root
    log_decay = math.log(decay_ratio)
    scaling = 1.0 / (
        big_root
        * (1.0 - decay_ratio * decay_ratio)
        * (1.0 - math.exp(2.0 * log_decay * (length + 1)))
    )
    return (log_decay, scaling)


def green_table(row_pos, col_pos, length, diffusion):
    log_decay, scaling = decay_constants(diffusion, length)
    nearer = jnp.minimum(row_pos, col_pos)
    farther = jnp.maximum(row_pos, col_pos)
    return (
        scaling
        * jnp.exp((farther - nearer) * log_decay)
        * -jnp.expm1((nearer + 1.0) * (2.0 * log_decay))
        * -jnp.expm1((length - farther) * (2.0 * log_decay))
    )


def explicit_local(values, line_dim, diffusion):
    length = values.shape[line_dim]
    zeros_rim = jnp.zeros_like(lax.slice_in_dim(values, 0, 1, axis=line_dim))
    before = jnp.concatenate(
        [zeros_rim, lax.slice_in_dim(values, 0, length - 1, axis=line_dim)], axis=line_dim
    )
    behind = jnp.concatenate(
        [lax.slice_in_dim(values, 1, length, axis=line_dim), zeros_rim], axis=line_dim
    )
    return (1.0 - 2.4 * diffusion) * values + (0.1 + 1.2 * diffusion) * (before + behind)


def line_solve(values, line_dim, diffusion, block_len):
    length = values.shape[line_dim]
    pieces = length // block_len
    couple = 1.2 * diffusion - 0.1
    within = jnp.arange(block_len, dtype=jnp.float32)
    local_inverse = green_table(within[:, None], within[None, :], block_len, diffusion)
    piece_pos = jnp.arange(pieces, dtype=jnp.float32)
    side_pos = jnp.arange(2, dtype=jnp.float32)
    row_pos = piece_pos[:, None, None, None] * block_len + within[None, :, None, None]
    col_pos = (
        piece_pos[None, None, :, None] * block_len
        - 1.0
        + side_pos[None, None, None, :] * (block_len + 1.0)
    )
    coupling = couple * green_table(row_pos, col_pos, length, diffusion)
    if line_dim == 2:
        lead_len, tail_len = (values.shape[0], values.shape[1])
        splitted = values.reshape(lead_len, tail_len, pieces, block_len)
        solved = jnp.einsum("abqj,ij->abqi", splitted, local_inverse, precision=HIGHEST)
        rim_values = jnp.stack([solved[..., 0], solved[..., block_len - 1]], axis=-1)
        corrected = solved + jnp.einsum("abks,qiks->abqi", rim_values, coupling, precision=HIGHEST)
        return corrected.reshape(lead_len, tail_len, length)
    lead_len, tail_len = (values.shape[0], values.shape[2])
    splitted = values.reshape(lead_len, pieces, block_len, tail_len)
    solved = jnp.einsum("aqjb,ij->aqib", splitted, local_inverse, precision=HIGHEST)
    rim_values = jnp.stack([solved[:, :, 0, :], solved[:, :, block_len - 1, :]], axis=2)
    corrected = solved + jnp.einsum("aksb,qiks->aqib", rim_values, coupling, precision=HIGHEST)
    return corrected.reshape(lead_len, length, tail_len)


def shifted(values, axis, step):
    count = lax.axis_size(axis)
    if step > 0:
        pairs = [(i, i + step) for i in range(count - step)]
    else:
        pairs = [(i - step, i) for i in range(count + step)]
    return lax.ppermute(values, axis, pairs)


def butterfly_scans(left, right, axis, ratio):
    count = lax.axis_size(axis)
    assert count & (count - 1) == 0
    me = lax.axis_index(axis)
    left_total, right_total = left, right
    left_excl = jnp.zeros_like(left)
    right_excl = jnp.zeros_like(right)
    half = 1
    while half < count:
        pairs = [(i, i ^ half) for i in range(count)]
        got = lax.ppermute(jnp.stack([left_total, right_total]), axis, pairs)
        upper = (me & half) != 0
        base = me - (me % (2 * half))
        mid_gap = (me - base - half).astype(jnp.float32)
        low_gap = (base + half - 1 - me).astype(jnp.float32)
        left_gain = jnp.where(upper, jnp.exp(mid_gap * math.log(ratio)), 0.0)
        right_gain = jnp.where(upper, 0.0, jnp.exp(low_gap * math.log(ratio)))
        left_excl = left_excl + left_gain * got[0]
        right_excl = right_excl + right_gain * got[1]
        decay = ratio ** half
        left_total = jnp.where(upper, left_total + decay * got[0], decay * left_total + got[0])
        right_total = jnp.where(upper, got[1] + decay * right_total, right_total + decay * got[1])
        half *= 2
    return left_excl, right_excl


def y_solve(along_x, head, tail, diffusion):
    y_rows = along_x.shape[0]
    before = lax.ppermute(tail, "gy", [(i, i + 1) for i in range(lax.axis_size("gy") - 1)])
    behind = lax.ppermute(head, "gy", [(i + 1, i) for i in range(lax.axis_size("gy") - 1)])
    padded = jnp.concatenate([before, along_x, behind], axis=0)
    rhs_y = (1.0 - 2.4 * diffusion) * along_x + (0.1 + 1.2 * diffusion) * (padded[:-2] + padded[2:])
    within = jnp.arange(y_rows, dtype=jnp.float32)
    local_inverse = green_table(within[:, None], within[None, :], y_rows, diffusion)
    rim_inverse = jnp.stack([local_inverse[0], local_inverse[y_rows - 1]])
    rims = jnp.einsum("ij,jzx->izx", rim_inverse, rhs_y, precision=HIGHEST)
    solved = lax.optimization_barrier(
        jnp.einsum("ij,jzx->izx", local_inverse, rhs_y, precision=HIGHEST)
    )
    first, last = rims[0], rims[1]

    devices = lax.axis_size("gy")
    length = devices * y_rows
    log_decay, scaling = decay_constants(diffusion, length)
    ratio = math.exp(log_decay)
    block_ratio = math.exp(log_decay * y_rows)
    couple = 1.2 * diffusion - 0.1
    start = lax.axis_index("gy").astype(jnp.float32) * y_rows

    def one_minus(power):
        return -jnp.expm1(power * (2.0 * log_decay))

    lead_first = one_minus(start)
    tail_last = one_minus(length - start - y_rows)
    left_part = ratio ** (y_rows + 1) * lead_first * first + one_minus(start + y_rows + 1) * last
    right_part = one_minus(length - start + 1) * first + ratio ** (y_rows + 1) * tail_last * last
    left_excl, right_excl = butterfly_scans(left_part, right_part, "gy", block_ratio)
    left_sum = left_excl + ratio * lead_first * first
    right_sum = right_excl + ratio * tail_last * last

    row_pos = start + within
    left_gain = (couple * scaling) * one_minus(length - row_pos) * jnp.exp(within * log_decay)
    right_gain = (couple * scaling) * one_minus(row_pos + 1.0) * jnp.exp((y_rows - 1.0 - within) * log_decay)
    return solved + left_gain[:, None, None] * left_sum[None] + right_gain[:, None, None] * right_sum[None]


def explicit_full(values, line_dim, diffusion):
    width = [(0, 0)] * values.ndim
    width[line_dim] = (1, 1)
    padded = jnp.pad(values, width)
    length = values.shape[line_dim]
    before = lax.slice_in_dim(padded, 0, length, axis=line_dim)
    behind = lax.slice_in_dim(padded, 2, length + 2, axis=line_dim)
    return (1.0 - 2.4 * diffusion) * values + (0.1 + 1.2 * diffusion) * (before + behind)


def full_inverse(length, diffusion):
    pos = jnp.arange(length, dtype=jnp.float32)
    return green_table(pos[:, None], pos[None, :], length, diffusion)


def x_solve(values, diffusion):
    inverse = full_inverse(values.shape[2], diffusion)
    return jnp.einsum("azj,ij->azi", explicit_full(values, 2, diffusion), inverse, precision=HIGHEST)


def z_solve(values, diffusion):
    inverse = full_inverse(values.shape[1], diffusion)
    return jnp.einsum("ij,ajx->aix", inverse, explicit_full(values, 1, diffusion), precision=HIGHEST)


def per_device(field):
    diffusion = float(LAMBDA)
    y_rows = field.shape[0]
    edges = jnp.stack([field[0], field[y_rows - 1]])
    edge_x = x_solve(edges, diffusion)
    along_x = x_solve(field, diffusion)
    along_y = y_solve(along_x, edge_x[0:1], edge_x[1:2], diffusion)
    pencils = lax.all_to_all(along_y, "gz", split_axis=0, concat_axis=1, tiled=True)
    return line_solve(explicit_local(pencils, 1, diffusion), 1, diffusion, BLK)


def solution(mesh):
    placed = (P("gy", "gz", None),)
    return jax.shard_map(
        per_device,
        mesh=mesh,
        in_specs=placed,
        out_specs=P(("gy", "gz"), None, None),
        check_vma=False,
    )
```

```python
import math

import jax
import jax.numpy as jnp
from jax import lax
from jax.sharding import PartitionSpec as P

BLK = 128
LAMBDA = 9216


HIGHEST = lax.Precision.HIGHEST


def padded_2(cells, sides, width):
    for axis, dim in sides:
        count = lax.axis_size(axis)
        ends = count - 1
        head = lax.slice_in_dim(cells, 0, width, axis=dim)
        tail = lax.slice_in_dim(cells, cells.shape[dim] - width, cells.shape[dim], axis=dim)
        cells = jnp.concatenate(
            [
                lax.ppermute(tail, axis, [(i, (i + 1) % count) for i in range(ends)]),
                cells,
                lax.ppermute(head, axis, [((i + 1) % count, i) for i in range(ends)]),
            ],
            axis=dim,
        )
    return cells


def decay_constants(diffusion, length):
    diagonal = 1.0 + 2.4 * diffusion
    off_diag = 0.1 - 1.2 * diffusion
    big_root = 0.5 * (diagonal + math.sqrt(diagonal * diagonal - 4.0 * off_diag * off_diag))
    decay_ratio = -off_diag / big_root
    log_decay = math.log(decay_ratio)
    scaling = 1.0 / (
        big_root
        * (1.0 - decay_ratio * decay_ratio)
        * (1.0 - math.exp(2.0 * log_decay * (length + 1)))
    )
    return (log_decay, scaling)


def green_table(row_pos, col_pos, length, diffusion):
    log_decay, scaling = decay_constants(diffusion, length)
    nearer = jnp.minimum(row_pos, col_pos)
    farther = jnp.maximum(row_pos, col_pos)
    return (
        scaling
        * jnp.exp((farther - nearer) * log_decay)
        * -jnp.expm1((nearer + 1.0) * (2.0 * log_decay))
        * -jnp.expm1((length - farther) * (2.0 * log_decay))
    )


def explicit_local(values, line_dim, diffusion):
    length = values.shape[line_dim]
    zeros_rim = jnp.zeros_like(lax.slice_in_dim(values, 0, 1, axis=line_dim))
    before = jnp.concatenate(
        [zeros_rim, lax.slice_in_dim(values, 0, length - 1, axis=line_dim)], axis=line_dim
    )
    behind = jnp.concatenate(
        [lax.slice_in_dim(values, 1, length, axis=line_dim), zeros_rim], axis=line_dim
    )
    return (1.0 - 2.4 * diffusion) * values + (0.1 + 1.2 * diffusion) * (before + behind)


def line_solve(values, line_dim, diffusion, block_len):
    length = values.shape[line_dim]
    pieces = length // block_len
    couple = 1.2 * diffusion - 0.1
    within = jnp.arange(block_len, dtype=jnp.float32)
    local_inverse = green_table(within[:, None], within[None, :], block_len, diffusion)
    piece_pos = jnp.arange(pieces, dtype=jnp.float32)
    side_pos = jnp.arange(2, dtype=jnp.float32)
    row_pos = piece_pos[:, None, None, None] * block_len + within[None, :, None, None]
    col_pos = (
        piece_pos[None, None, :, None] * block_len
        - 1.0
        + side_pos[None, None, None, :] * (block_len + 1.0)
    )
    coupling = couple * green_table(row_pos, col_pos, length, diffusion)
    if line_dim == 2:
        lead_len, tail_len = (values.shape[0], values.shape[1])
        splitted = values.reshape(lead_len, tail_len, pieces, block_len)
        solved = jnp.einsum("abqj,ij->abqi", splitted, local_inverse, precision=HIGHEST)
        rim_values = jnp.stack([solved[..., 0], solved[..., block_len - 1]], axis=-1)
        corrected = solved + jnp.einsum("abks,qiks->abqi", rim_values, coupling, precision=HIGHEST)
        return corrected.reshape(lead_len, tail_len, length)
    lead_len, tail_len = (values.shape[0], values.shape[2])
    splitted = values.reshape(lead_len, pieces, block_len, tail_len)
    solved = jnp.einsum("aqjb,ij->aqib", splitted, local_inverse, precision=HIGHEST)
    rim_values = jnp.stack([solved[:, :, 0, :], solved[:, :, block_len - 1, :]], axis=2)
    corrected = solved + jnp.einsum("aksb,qiks->aqib", rim_values, coupling, precision=HIGHEST)
    return corrected.reshape(lead_len, length, tail_len)


def shifted(values, axis, step):
    count = lax.axis_size(axis)
    if step > 0:
        pairs = [(i, i + step) for i in range(count - step)]
    else:
        pairs = [(i - step, i) for i in range(count + step)]
    return lax.ppermute(values, axis, pairs)


def butterfly_scans(left, right, axis, ratio):
    count = lax.axis_size(axis)
    assert count & (count - 1) == 0
    me = lax.axis_index(axis)
    left_total, right_total = left, right
    left_excl = jnp.zeros_like(left)
    right_excl = jnp.zeros_like(right)
    half = 1
    while half < count:
        pairs = [(i, i ^ half) for i in range(count)]
        got = lax.ppermute(jnp.stack([left_total, right_total]), axis, pairs)
        upper = (me & half) != 0
        base = me - (me % (2 * half))
        mid_gap = (me - base - half).astype(jnp.float32)
        low_gap = (base + half - 1 - me).astype(jnp.float32)
        left_gain = jnp.where(upper, jnp.exp(mid_gap * math.log(ratio)), 0.0)
        right_gain = jnp.where(upper, 0.0, jnp.exp(low_gap * math.log(ratio)))
        left_excl = left_excl + left_gain * got[0]
        right_excl = right_excl + right_gain * got[1]
        decay = ratio ** half
        left_total = jnp.where(upper, left_total + decay * got[0], decay * left_total + got[0])
        right_total = jnp.where(upper, got[1] + decay * right_total, right_total + decay * got[1])
        half *= 2
    return left_excl, right_excl


def y_solve(along_x, head, tail, diffusion):
    y_rows = along_x.shape[0]
    before = lax.ppermute(tail, "gy", [(i, i + 1) for i in range(lax.axis_size("gy") - 1)])
    behind = lax.ppermute(head, "gy", [(i + 1, i) for i in range(lax.axis_size("gy") - 1)])
    padded = jnp.concatenate([before, along_x, behind], axis=0)
    rhs_y = (1.0 - 2.4 * diffusion) * along_x + (0.1 + 1.2 * diffusion) * (padded[:-2] + padded[2:])
    within = jnp.arange(y_rows, dtype=jnp.float32)
    local_inverse = green_table(within[:, None], within[None, :], y_rows, diffusion)
    rim_inverse = jnp.stack([local_inverse[0], local_inverse[y_rows - 1]])
    rims = jnp.einsum("ij,jzx->izx", rim_inverse, rhs_y, precision=HIGHEST)
    solved = jnp.einsum("ij,jzx->izx", local_inverse, rhs_y, precision=HIGHEST)
    first, last = rims[0], rims[1]

    devices = lax.axis_size("gy")
    length = devices * y_rows
    log_decay, scaling = decay_constants(diffusion, length)
    ratio = math.exp(log_decay)
    block_ratio = math.exp(log_decay * y_rows)
    couple = 1.2 * diffusion - 0.1
    start = lax.axis_index("gy").astype(jnp.float32) * y_rows

    def one_minus(power):
        return -jnp.expm1(power * (2.0 * log_decay))

    lead_first = one_minus(start)
    tail_last = one_minus(length - start - y_rows)
    left_part = ratio ** (y_rows + 1) * lead_first * first + one_minus(start + y_rows + 1) * last
    right_part = one_minus(length - start + 1) * first + ratio ** (y_rows + 1) * tail_last * last
    left_excl, right_excl = butterfly_scans(left_part, right_part, "gy", block_ratio)
    left_sum = left_excl + ratio * lead_first * first
    right_sum = right_excl + ratio * tail_last * last

    moved = lax.all_to_all(solved, "gz", split_axis=0, concat_axis=1, tiled=True)
    sums = lax.all_gather(jnp.stack([left_sum, right_sum]), "gz", axis=1, tiled=True)
    rows_here = moved.shape[0]
    offset = lax.axis_index("gz").astype(jnp.float32) * rows_here
    within_here = offset + jnp.arange(rows_here, dtype=jnp.float32)
    row_pos = start + within_here
    left_gain = (couple * scaling) * one_minus(length - row_pos) * jnp.exp(within_here * log_decay)
    right_gain = (couple * scaling) * one_minus(row_pos + 1.0) * jnp.exp((y_rows - 1.0 - within_here) * log_decay)
    return moved + left_gain[:, None, None] * sums[0][None] + right_gain[:, None, None] * sums[1][None]


def explicit_full(values, line_dim, diffusion):
    width = [(0, 0)] * values.ndim
    width[line_dim] = (1, 1)
    padded = jnp.pad(values, width)
    length = values.shape[line_dim]
    before = lax.slice_in_dim(padded, 0, length, axis=line_dim)
    behind = lax.slice_in_dim(padded, 2, length + 2, axis=line_dim)
    return (1.0 - 2.4 * diffusion) * values + (0.1 + 1.2 * diffusion) * (before + behind)


def full_inverse(length, diffusion):
    pos = jnp.arange(length, dtype=jnp.float32)
    return green_table(pos[:, None], pos[None, :], length, diffusion)


def x_solve(values, diffusion):
    inverse = full_inverse(values.shape[2], diffusion)
    return jnp.einsum("azj,ij->azi", explicit_full(values, 2, diffusion), inverse, precision=HIGHEST)


def z_solve(values, diffusion):
    inverse = full_inverse(values.shape[1], diffusion)
    return jnp.einsum("ij,ajx->aix", inverse, explicit_full(values, 1, diffusion), precision=HIGHEST)


def per_device(field):
    diffusion = float(LAMBDA)
    y_rows = field.shape[0]
    edges = jnp.stack([field[0], field[y_rows - 1]])
    edge_x = x_solve(edges, diffusion)
    along_x = x_solve(field, diffusion)
    along_y = y_solve(along_x, edge_x[0:1], edge_x[1:2], diffusion)
    return line_solve(explicit_local(along_y, 1, diffusion), 1, diffusion, BLK)


def solution(mesh):
    placed = (P("gy", "gz", None),)
    return jax.shard_map(
        per_device,
        mesh=mesh,
        in_specs=placed,
        out_specs=P(("gy", "gz"), None, None),
        check_vma=False,
    )
```

```python
import math

import jax
import jax.numpy as jnp
from jax import lax
from jax.sharding import PartitionSpec as P

BLK = 128
LAMBDA = 9216


HIGHEST = lax.Precision.HIGHEST


def padded_2(cells, sides, width):
    for axis, dim in sides:
        count = lax.axis_size(axis)
        ends = count - 1
        head = lax.slice_in_dim(cells, 0, width, axis=dim)
        tail = lax.slice_in_dim(cells, cells.shape[dim] - width, cells.shape[dim], axis=dim)
        cells = jnp.concatenate(
            [
                lax.ppermute(tail, axis, [(i, (i + 1) % count) for i in range(ends)]),
                cells,
                lax.ppermute(head, axis, [((i + 1) % count, i) for i in range(ends)]),
            ],
            axis=dim,
        )
    return cells


def decay_constants(diffusion, length):
    diagonal = 1.0 + 2.4 * diffusion
    off_diag = 0.1 - 1.2 * diffusion
    big_root = 0.5 * (diagonal + math.sqrt(diagonal * diagonal - 4.0 * off_diag * off_diag))
    decay_ratio = -off_diag / big_root
    log_decay = math.log(decay_ratio)
    scaling = 1.0 / (
        big_root
        * (1.0 - decay_ratio * decay_ratio)
        * (1.0 - math.exp(2.0 * log_decay * (length + 1)))
    )
    return (log_decay, scaling)


def green_table(row_pos, col_pos, length, diffusion):
    log_decay, scaling = decay_constants(diffusion, length)
    nearer = jnp.minimum(row_pos, col_pos)
    farther = jnp.maximum(row_pos, col_pos)
    return (
        scaling
        * jnp.exp((farther - nearer) * log_decay)
        * -jnp.expm1((nearer + 1.0) * (2.0 * log_decay))
        * -jnp.expm1((length - farther) * (2.0 * log_decay))
    )


def explicit_local(values, line_dim, diffusion):
    length = values.shape[line_dim]
    zeros_rim = jnp.zeros_like(lax.slice_in_dim(values, 0, 1, axis=line_dim))
    before = jnp.concatenate(
        [zeros_rim, lax.slice_in_dim(values, 0, length - 1, axis=line_dim)], axis=line_dim
    )
    behind = jnp.concatenate(
        [lax.slice_in_dim(values, 1, length, axis=line_dim), zeros_rim], axis=line_dim
    )
    return (1.0 - 2.4 * diffusion) * values + (0.1 + 1.2 * diffusion) * (before + behind)


def line_solve(values, line_dim, diffusion, block_len):
    length = values.shape[line_dim]
    pieces = length // block_len
    couple = 1.2 * diffusion - 0.1
    within = jnp.arange(block_len, dtype=jnp.float32)
    local_inverse = green_table(within[:, None], within[None, :], block_len, diffusion)
    piece_pos = jnp.arange(pieces, dtype=jnp.float32)
    side_pos = jnp.arange(2, dtype=jnp.float32)
    row_pos = piece_pos[:, None, None, None] * block_len + within[None, :, None, None]
    col_pos = (
        piece_pos[None, None, :, None] * block_len
        - 1.0
        + side_pos[None, None, None, :] * (block_len + 1.0)
    )
    coupling = couple * green_table(row_pos, col_pos, length, diffusion)
    if line_dim == 2:
        lead_len, tail_len = (values.shape[0], values.shape[1])
        splitted = values.reshape(lead_len, tail_len, pieces, block_len)
        solved = jnp.einsum("abqj,ij->abqi", splitted, local_inverse, precision=HIGHEST)
        rim_values = jnp.stack([solved[..., 0], solved[..., block_len - 1]], axis=-1)
        corrected = solved + jnp.einsum("abks,qiks->abqi", rim_values, coupling, precision=HIGHEST)
        return corrected.reshape(lead_len, tail_len, length)
    lead_len, tail_len = (values.shape[0], values.shape[2])
    splitted = values.reshape(lead_len, pieces, block_len, tail_len)
    solved = jnp.einsum("aqjb,ij->aqib", splitted, local_inverse, precision=HIGHEST)
    rim_values = jnp.stack([solved[:, :, 0, :], solved[:, :, block_len - 1, :]], axis=2)
    corrected = solved + jnp.einsum("aksb,qiks->aqib", rim_values, coupling, precision=HIGHEST)
    return corrected.reshape(lead_len, length, tail_len)


def shifted(values, axis, step):
    count = lax.axis_size(axis)
    if step > 0:
        pairs = [(i, i + step) for i in range(count - step)]
    else:
        pairs = [(i - step, i) for i in range(count + step)]
    return lax.ppermute(values, axis, pairs)


def butterfly_scans(left, right, axis, ratio):
    count = lax.axis_size(axis)
    assert count & (count - 1) == 0
    me = lax.axis_index(axis)
    left_total, right_total = left, right
    left_excl = jnp.zeros_like(left)
    right_excl = jnp.zeros_like(right)
    half = 1
    while half < count:
        pairs = [(i, i ^ half) for i in range(count)]
        got = lax.ppermute(jnp.stack([left_total, right_total]), axis, pairs)
        upper = (me & half) != 0
        base = me - (me % (2 * half))
        mid_gap = (me - base - half).astype(jnp.float32)
        low_gap = (base + half - 1 - me).astype(jnp.float32)
        left_gain = jnp.where(upper, jnp.exp(mid_gap * math.log(ratio)), 0.0)
        right_gain = jnp.where(upper, 0.0, jnp.exp(low_gap * math.log(ratio)))
        left_excl = left_excl + left_gain * got[0]
        right_excl = right_excl + right_gain * got[1]
        decay = ratio ** half
        left_total = jnp.where(upper, left_total + decay * got[0], decay * left_total + got[0])
        right_total = jnp.where(upper, got[1] + decay * right_total, right_total + decay * got[1])
        half *= 2
    return left_excl, right_excl


def y_solve(along_x, head, tail, diffusion):
    y_rows = along_x.shape[0]
    before = lax.ppermute(tail, "gy", [(i, i + 1) for i in range(lax.axis_size("gy") - 1)])
    behind = lax.ppermute(head, "gy", [(i + 1, i) for i in range(lax.axis_size("gy") - 1)])
    within = jnp.arange(y_rows, dtype=jnp.float32)
    local_inverse = green_table(within[:, None], within[None, :], y_rows, diffusion)
    side = 0.1 + 1.2 * diffusion
    shift_sum = jnp.eye(y_rows, k=1, dtype=jnp.float32) + jnp.eye(y_rows, k=-1, dtype=jnp.float32)
    explicit = (1.0 - 2.4 * diffusion) * jnp.eye(y_rows, dtype=jnp.float32) + side * shift_sum
    combined = jnp.dot(local_inverse, explicit, precision=HIGHEST)
    enter = side * local_inverse[:, 0]
    leave = side * local_inverse[:, y_rows - 1]

    def apply(rows, weights):
        picked = jnp.einsum("ij,jzx->izx", weights[rows], along_x, precision=HIGHEST)
        return picked + enter[rows][:, None, None] * before + leave[rows][:, None, None] * behind

    rims = apply(jnp.array([0, y_rows - 1]), combined)
    solved = lax.optimization_barrier(apply(jnp.arange(y_rows), combined))
    first, last = rims[0], rims[1]

    devices = lax.axis_size("gy")
    length = devices * y_rows
    log_decay, scaling = decay_constants(diffusion, length)
    ratio = math.exp(log_decay)
    block_ratio = math.exp(log_decay * y_rows)
    couple = 1.2 * diffusion - 0.1
    start = lax.axis_index("gy").astype(jnp.float32) * y_rows

    def one_minus(power):
        return -jnp.expm1(power * (2.0 * log_decay))

    lead_first = one_minus(start)
    tail_last = one_minus(length - start - y_rows)
    left_part = ratio ** (y_rows + 1) * lead_first * first + one_minus(start + y_rows + 1) * last
    right_part = one_minus(length - start + 1) * first + ratio ** (y_rows + 1) * tail_last * last
    left_excl, right_excl = butterfly_scans(left_part, right_part, "gy", block_ratio)
    left_sum = left_excl + ratio * lead_first * first
    right_sum = right_excl + ratio * tail_last * last

    row_pos = start + within
    left_gain = (couple * scaling) * one_minus(length - row_pos) * jnp.exp(within * log_decay)
    right_gain = (couple * scaling) * one_minus(row_pos + 1.0) * jnp.exp((y_rows - 1.0 - within) * log_decay)
    return solved + left_gain[:, None, None] * left_sum[None] + right_gain[:, None, None] * right_sum[None]


def explicit_full(values, line_dim, diffusion):
    width = [(0, 0)] * values.ndim
    width[line_dim] = (1, 1)
    padded = jnp.pad(values, width)
    length = values.shape[line_dim]
    before = lax.slice_in_dim(padded, 0, length, axis=line_dim)
    behind = lax.slice_in_dim(padded, 2, length + 2, axis=line_dim)
    return (1.0 - 2.4 * diffusion) * values + (0.1 + 1.2 * diffusion) * (before + behind)


def full_inverse(length, diffusion):
    pos = jnp.arange(length, dtype=jnp.float32)
    return green_table(pos[:, None], pos[None, :], length, diffusion)


def x_solve(values, diffusion):
    inverse = full_inverse(values.shape[2], diffusion)
    return jnp.einsum("azj,ij->azi", explicit_full(values, 2, diffusion), inverse, precision=HIGHEST)


def z_solve(values, diffusion):
    inverse = full_inverse(values.shape[1], diffusion)
    return jnp.einsum("ij,ajx->aix", inverse, explicit_full(values, 1, diffusion), precision=HIGHEST)


CHUNKS = 2


def per_device(field):
    diffusion = float(LAMBDA)
    y_rows = field.shape[0]
    edges = jnp.stack([field[0], field[y_rows - 1]])
    edge_x = x_solve(edges, diffusion)
    along_x = x_solve(field, diffusion)
    along_y = y_solve(along_x, edge_x[0:1], edge_x[1:2], diffusion)
    width = along_y.shape[2] // CHUNKS
    parts = []
    for k in range(CHUNKS):
        piece = along_y[:, :, k * width:(k + 1) * width]
        pencils = lax.all_to_all(piece, "gz", split_axis=0, concat_axis=1, tiled=True)
        parts.append(z_solve(pencils, diffusion))
    return jnp.concatenate(parts, axis=2)


def solution(mesh):
    placed = (P("gy", "gz", None),)
    return jax.shard_map(
        per_device,
        mesh=mesh,
        in_specs=placed,
        out_specs=P(("gy", "gz"), None, None),
        check_vma=False,
    )
```

```python
import math

import jax
import jax.numpy as jnp
from jax import lax
from jax.sharding import PartitionSpec as P

BLK = 128
LAMBDA = 9216


HIGHEST = lax.Precision.HIGHEST


def padded_2(cells, sides, width):
    for axis, dim in sides:
        count = lax.axis_size(axis)
        ends = count - 1
        head = lax.slice_in_dim(cells, 0, width, axis=dim)
        tail = lax.slice_in_dim(cells, cells.shape[dim] - width, cells.shape[dim], axis=dim)
        cells = jnp.concatenate(
            [
                lax.ppermute(tail, axis, [(i, (i + 1) % count) for i in range(ends)]),
                cells,
                lax.ppermute(head, axis, [((i + 1) % count, i) for i in range(ends)]),
            ],
            axis=dim,
        )
    return cells


def decay_constants(diffusion, length):
    diagonal = 1.0 + 2.4 * diffusion
    off_diag = 0.1 - 1.2 * diffusion
    big_root = 0.5 * (diagonal + math.sqrt(diagonal * diagonal - 4.0 * off_diag * off_diag))
    decay_ratio = -off_diag / big_root
    log_decay = math.log(decay_ratio)
    scaling = 1.0 / (
        big_root
        * (1.0 - decay_ratio * decay_ratio)
        * (1.0 - math.exp(2.0 * log_decay * (length + 1)))
    )
    return (log_decay, scaling)


def green_table(row_pos, col_pos, length, diffusion):
    log_decay, scaling = decay_constants(diffusion, length)
    nearer = jnp.minimum(row_pos, col_pos)
    farther = jnp.maximum(row_pos, col_pos)
    return (
        scaling
        * jnp.exp((farther - nearer) * log_decay)
        * -jnp.expm1((nearer + 1.0) * (2.0 * log_decay))
        * -jnp.expm1((length - farther) * (2.0 * log_decay))
    )


def explicit_local(values, line_dim, diffusion):
    length = values.shape[line_dim]
    zeros_rim = jnp.zeros_like(lax.slice_in_dim(values, 0, 1, axis=line_dim))
    before = jnp.concatenate(
        [zeros_rim, lax.slice_in_dim(values, 0, length - 1, axis=line_dim)], axis=line_dim
    )
    behind = jnp.concatenate(
        [lax.slice_in_dim(values, 1, length, axis=line_dim), zeros_rim], axis=line_dim
    )
    return (1.0 - 2.4 * diffusion) * values + (0.1 + 1.2 * diffusion) * (before + behind)


def line_solve(values, line_dim, diffusion, block_len):
    length = values.shape[line_dim]
    pieces = length // block_len
    couple = 1.2 * diffusion - 0.1
    within = jnp.arange(block_len, dtype=jnp.float32)
    local_inverse = green_table(within[:, None], within[None, :], block_len, diffusion)
    piece_pos = jnp.arange(pieces, dtype=jnp.float32)
    side_pos = jnp.arange(2, dtype=jnp.float32)
    row_pos = piece_pos[:, None, None, None] * block_len + within[None, :, None, None]
    col_pos = (
        piece_pos[None, None, :, None] * block_len
        - 1.0
        + side_pos[None, None, None, :] * (block_len + 1.0)
    )
    coupling = couple * green_table(row_pos, col_pos, length, diffusion)
    if line_dim == 2:
        lead_len, tail_len = (values.shape[0], values.shape[1])
        splitted = values.reshape(lead_len, tail_len, pieces, block_len)
        solved = jnp.einsum("abqj,ij->abqi", splitted, local_inverse, precision=HIGHEST)
        rim_values = jnp.stack([solved[..., 0], solved[..., block_len - 1]], axis=-1)
        corrected = solved + jnp.einsum("abks,qiks->abqi", rim_values, coupling, precision=HIGHEST)
        return corrected.reshape(lead_len, tail_len, length)
    lead_len, tail_len = (values.shape[0], values.shape[2])
    splitted = values.reshape(lead_len, pieces, block_len, tail_len)
    solved = jnp.einsum("aqjb,ij->aqib", splitted, local_inverse, precision=HIGHEST)
    rim_values = jnp.stack([solved[:, :, 0, :], solved[:, :, block_len - 1, :]], axis=2)
    corrected = solved + jnp.einsum("aksb,qiks->aqib", rim_values, coupling, precision=HIGHEST)
    return corrected.reshape(lead_len, length, tail_len)


def shifted(values, axis, step):
    count = lax.axis_size(axis)
    if step > 0:
        pairs = [(i, i + step) for i in range(count - step)]
    else:
        pairs = [(i - step, i) for i in range(count + step)]
    return lax.ppermute(values, axis, pairs)


def butterfly_scans(left, right, axis, ratio):
    count = lax.axis_size(axis)
    assert count & (count - 1) == 0
    me = lax.axis_index(axis)
    left_total, right_total = left, right
    left_excl = jnp.zeros_like(left)
    right_excl = jnp.zeros_like(right)
    half = 1
    while half < count:
        pairs = [(i, i ^ half) for i in range(count)]
        got = lax.ppermute(jnp.stack([left_total, right_total]), axis, pairs)
        upper = (me & half) != 0
        base = me - (me % (2 * half))
        mid_gap = (me - base - half).astype(jnp.float32)
        low_gap = (base + half - 1 - me).astype(jnp.float32)
        left_gain = jnp.where(upper, jnp.exp(mid_gap * math.log(ratio)), 0.0)
        right_gain = jnp.where(upper, 0.0, jnp.exp(low_gap * math.log(ratio)))
        left_excl = left_excl + left_gain * got[0]
        right_excl = right_excl + right_gain * got[1]
        decay = ratio ** half
        left_total = jnp.where(upper, left_total + decay * got[0], decay * left_total + got[0])
        right_total = jnp.where(upper, got[1] + decay * right_total, right_total + decay * got[1])
        half *= 2
    return left_excl, right_excl


def y_solve(along_x, head, tail, diffusion):
    y_rows = along_x.shape[0]
    before = lax.ppermute(tail, "gy", [(i, i + 1) for i in range(lax.axis_size("gy") - 1)])
    behind = lax.ppermute(head, "gy", [(i + 1, i) for i in range(lax.axis_size("gy") - 1)])
    within = jnp.arange(y_rows, dtype=jnp.float32)
    local_inverse = green_table(within[:, None], within[None, :], y_rows, diffusion)
    side = 0.1 + 1.2 * diffusion
    shift_sum = jnp.eye(y_rows, k=1, dtype=jnp.float32) + jnp.eye(y_rows, k=-1, dtype=jnp.float32)
    explicit = (1.0 - 2.4 * diffusion) * jnp.eye(y_rows, dtype=jnp.float32) + side * shift_sum
    combined = jnp.dot(local_inverse, explicit, precision=HIGHEST)
    enter = side * local_inverse[:, 0]
    leave = side * local_inverse[:, y_rows - 1]

    def apply(rows, weights):
        picked = jnp.einsum("ij,jzx->izx", weights[rows], along_x, precision=HIGHEST)
        return picked + enter[rows][:, None, None] * before + leave[rows][:, None, None] * behind

    rims = apply(jnp.array([0, y_rows - 1]), combined)
    solved = lax.optimization_barrier(apply(jnp.arange(y_rows), combined))
    first, last = rims[0], rims[1]

    devices = lax.axis_size("gy")
    length = devices * y_rows
    log_decay, scaling = decay_constants(diffusion, length)
    ratio = math.exp(log_decay)
    block_ratio = math.exp(log_decay * y_rows)
    couple = 1.2 * diffusion - 0.1
    start = lax.axis_index("gy").astype(jnp.float32) * y_rows

    def one_minus(power):
        return -jnp.expm1(power * (2.0 * log_decay))

    lead_first = one_minus(start)
    tail_last = one_minus(length - start - y_rows)
    left_part = ratio ** (y_rows + 1) * lead_first * first + one_minus(start + y_rows + 1) * last
    right_part = one_minus(length - start + 1) * first + ratio ** (y_rows + 1) * tail_last * last
    left_excl, right_excl = butterfly_scans(left_part, right_part, "gy", block_ratio)
    left_sum = left_excl + ratio * lead_first * first
    right_sum = right_excl + ratio * tail_last * last

    row_pos = start + within
    left_gain = (couple * scaling) * one_minus(length - row_pos) * jnp.exp(within * log_decay)
    right_gain = (couple * scaling) * one_minus(row_pos + 1.0) * jnp.exp((y_rows - 1.0 - within) * log_decay)
    return solved + left_gain[:, None, None] * left_sum[None] + right_gain[:, None, None] * right_sum[None]


def explicit_full(values, line_dim, diffusion):
    width = [(0, 0)] * values.ndim
    width[line_dim] = (1, 1)
    padded = jnp.pad(values, width)
    length = values.shape[line_dim]
    before = lax.slice_in_dim(padded, 0, length, axis=line_dim)
    behind = lax.slice_in_dim(padded, 2, length + 2, axis=line_dim)
    return (1.0 - 2.4 * diffusion) * values + (0.1 + 1.2 * diffusion) * (before + behind)


def full_inverse(length, diffusion):
    pos = jnp.arange(length, dtype=jnp.float32)
    return green_table(pos[:, None], pos[None, :], length, diffusion)


def folded_inverse(length, diffusion):
    inverse = full_inverse(length, diffusion)
    shift_sum = jnp.eye(length, k=1, dtype=jnp.float32) + jnp.eye(length, k=-1, dtype=jnp.float32)
    explicit = (1.0 - 2.4 * diffusion) * jnp.eye(length, dtype=jnp.float32) + (0.1 + 1.2 * diffusion) * shift_sum
    return jnp.dot(inverse, explicit, precision=HIGHEST)


def x_solve(values, diffusion):
    combined = folded_inverse(values.shape[2], diffusion)
    return jnp.einsum("azj,ij->azi", values, combined, precision=HIGHEST)


def z_solve(values, diffusion):
    combined = folded_inverse(values.shape[1], diffusion)
    return jnp.einsum("ij,ajx->aix", combined, values, precision=HIGHEST)


CHUNKS = 2


def per_device(field):
    diffusion = float(LAMBDA)
    y_rows = field.shape[0]
    edges = jnp.stack([field[0], field[y_rows - 1]])
    edge_x = x_solve(edges, diffusion)
    along_x = x_solve(field, diffusion)
    along_y = y_solve(along_x, edge_x[0:1], edge_x[1:2], diffusion)
    width = along_y.shape[2] // CHUNKS
    parts = []
    for k in range(CHUNKS):
        piece = along_y[:, :, k * width:(k + 1) * width]
        pencils = lax.all_to_all(piece, "gz", split_axis=0, concat_axis=1, tiled=True)
        parts.append(z_solve(pencils, diffusion))
    return jnp.concatenate(parts, axis=2)


def solution(mesh):
    placed = (P("gy", "gz", None),)
    return jax.shard_map(
        per_device,
        mesh=mesh,
        in_specs=placed,
        out_specs=P(("gy", "gz"), None, None),
        check_vma=False,
    )
```

```python
import math

import jax
import jax.numpy as jnp
from jax import lax
from jax.sharding import PartitionSpec as P

BLK = 128
LAMBDA = 9216


HIGHEST = lax.Precision.HIGHEST


def padded_2(cells, sides, width):
    for axis, dim in sides:
        count = lax.axis_size(axis)
        ends = count - 1
        head = lax.slice_in_dim(cells, 0, width, axis=dim)
        tail = lax.slice_in_dim(cells, cells.shape[dim] - width, cells.shape[dim], axis=dim)
        cells = jnp.concatenate(
            [
                lax.ppermute(tail, axis, [(i, (i + 1) % count) for i in range(ends)]),
                cells,
                lax.ppermute(head, axis, [((i + 1) % count, i) for i in range(ends)]),
            ],
            axis=dim,
        )
    return cells


def decay_constants(diffusion, length):
    diagonal = 1.0 + 2.4 * diffusion
    off_diag = 0.1 - 1.2 * diffusion
    big_root = 0.5 * (diagonal + math.sqrt(diagonal * diagonal - 4.0 * off_diag * off_diag))
    decay_ratio = -off_diag / big_root
    log_decay = math.log(decay_ratio)
    scaling = 1.0 / (
        big_root
        * (1.0 - decay_ratio * decay_ratio)
        * (1.0 - math.exp(2.0 * log_decay * (length + 1)))
    )
    return (log_decay, scaling)


def green_table(row_pos, col_pos, length, diffusion):
    log_decay, scaling = decay_constants(diffusion, length)
    nearer = jnp.minimum(row_pos, col_pos)
    farther = jnp.maximum(row_pos, col_pos)
    return (
        scaling
        * jnp.exp((farther - nearer) * log_decay)
        * -jnp.expm1((nearer + 1.0) * (2.0 * log_decay))
        * -jnp.expm1((length - farther) * (2.0 * log_decay))
    )


def explicit_local(values, line_dim, diffusion):
    length = values.shape[line_dim]
    zeros_rim = jnp.zeros_like(lax.slice_in_dim(values, 0, 1, axis=line_dim))
    before = jnp.concatenate(
        [zeros_rim, lax.slice_in_dim(values, 0, length - 1, axis=line_dim)], axis=line_dim
    )
    behind = jnp.concatenate(
        [lax.slice_in_dim(values, 1, length, axis=line_dim), zeros_rim], axis=line_dim
    )
    return (1.0 - 2.4 * diffusion) * values + (0.1 + 1.2 * diffusion) * (before + behind)


def line_solve(values, line_dim, diffusion, block_len):
    length = values.shape[line_dim]
    pieces = length // block_len
    couple = 1.2 * diffusion - 0.1
    within = jnp.arange(block_len, dtype=jnp.float32)
    local_inverse = green_table(within[:, None], within[None, :], block_len, diffusion)
    piece_pos = jnp.arange(pieces, dtype=jnp.float32)
    side_pos = jnp.arange(2, dtype=jnp.float32)
    row_pos = piece_pos[:, None, None, None] * block_len + within[None, :, None, None]
    col_pos = (
        piece_pos[None, None, :, None] * block_len
        - 1.0
        + side_pos[None, None, None, :] * (block_len + 1.0)
    )
    coupling = couple * green_table(row_pos, col_pos, length, diffusion)
    if line_dim == 2:
        lead_len, tail_len = (values.shape[0], values.shape[1])
        splitted = values.reshape(lead_len, tail_len, pieces, block_len)
        solved = jnp.einsum("abqj,ij->abqi", splitted, local_inverse, precision=HIGHEST)
        rim_values = jnp.stack([solved[..., 0], solved[..., block_len - 1]], axis=-1)
        corrected = solved + jnp.einsum("abks,qiks->abqi", rim_values, coupling, precision=HIGHEST)
        return corrected.reshape(lead_len, tail_len, length)
    lead_len, tail_len = (values.shape[0], values.shape[2])
    splitted = values.reshape(lead_len, pieces, block_len, tail_len)
    solved = jnp.einsum("aqjb,ij->aqib", splitted, local_inverse, precision=HIGHEST)
    rim_values = jnp.stack([solved[:, :, 0, :], solved[:, :, block_len - 1, :]], axis=2)
    corrected = solved + jnp.einsum("aksb,qiks->aqib", rim_values, coupling, precision=HIGHEST)
    return corrected.reshape(lead_len, length, tail_len)


def shifted(values, axis, step):
    count = lax.axis_size(axis)
    if step > 0:
        pairs = [(i, i + step) for i in range(count - step)]
    else:
        pairs = [(i - step, i) for i in range(count + step)]
    return lax.ppermute(values, axis, pairs)


def butterfly_scans(left, right, axis, ratio):
    count = lax.axis_size(axis)
    assert count & (count - 1) == 0
    me = lax.axis_index(axis)
    left_total, right_total = left, right
    left_excl = jnp.zeros_like(left)
    right_excl = jnp.zeros_like(right)
    half = 1
    while half < count:
        pairs = [(i, i ^ half) for i in range(count)]
        got = lax.ppermute(jnp.stack([left_total, right_total]), axis, pairs)
        upper = (me & half) != 0
        base = me - (me % (2 * half))
        mid_gap = (me - base - half).astype(jnp.float32)
        low_gap = (base + half - 1 - me).astype(jnp.float32)
        left_gain = jnp.where(upper, jnp.exp(mid_gap * math.log(ratio)), 0.0)
        right_gain = jnp.where(upper, 0.0, jnp.exp(low_gap * math.log(ratio)))
        left_excl = left_excl + left_gain * got[0]
        right_excl = right_excl + right_gain * got[1]
        decay = ratio ** half
        left_total = jnp.where(upper, left_total + decay * got[0], decay * left_total + got[0])
        right_total = jnp.where(upper, got[1] + decay * right_total, right_total + decay * got[1])
        half *= 2
    return left_excl, right_excl


def y_solve(along_x, head, tail, diffusion):
    y_rows = along_x.shape[0]
    before = lax.ppermute(tail, "gy", [(i, i + 1) for i in range(lax.axis_size("gy") - 1)])
    behind = lax.ppermute(head, "gy", [(i + 1, i) for i in range(lax.axis_size("gy") - 1)])
    within = jnp.arange(y_rows, dtype=jnp.float32)
    local_inverse = green_table(within[:, None], within[None, :], y_rows, diffusion)
    side = 0.1 + 1.2 * diffusion
    shift_sum = jnp.eye(y_rows, k=1, dtype=jnp.float32) + jnp.eye(y_rows, k=-1, dtype=jnp.float32)
    explicit = (1.0 - 2.4 * diffusion) * jnp.eye(y_rows, dtype=jnp.float32) + side * shift_sum
    combined = jnp.dot(local_inverse, explicit, precision=HIGHEST)
    enter = side * local_inverse[:, 0]
    leave = side * local_inverse[:, y_rows - 1]

    def apply(rows, weights):
        picked = jnp.einsum("ij,jzx->izx", weights[rows], along_x, precision=HIGHEST)
        return picked + enter[rows][:, None, None] * before + leave[rows][:, None, None] * behind

    def rim(row):
        weighted = jnp.sum(combined[row][:, None, None] * along_x, axis=0)
        return weighted + enter[row] * before[0] + leave[row] * behind[0]

    rims = jnp.stack([rim(0), rim(y_rows - 1)])
    solved = lax.optimization_barrier(apply(jnp.arange(y_rows), combined))
    first, last = rims[0], rims[1]

    devices = lax.axis_size("gy")
    length = devices * y_rows
    log_decay, scaling = decay_constants(diffusion, length)
    ratio = math.exp(log_decay)
    block_ratio = math.exp(log_decay * y_rows)
    couple = 1.2 * diffusion - 0.1
    start = lax.axis_index("gy").astype(jnp.float32) * y_rows

    def one_minus(power):
        return -jnp.expm1(power * (2.0 * log_decay))

    lead_first = one_minus(start)
    tail_last = one_minus(length - start - y_rows)
    left_part = ratio ** (y_rows + 1) * lead_first * first + one_minus(start + y_rows + 1) * last
    right_part = one_minus(length - start + 1) * first + ratio ** (y_rows + 1) * tail_last * last
    left_excl, right_excl = butterfly_scans(left_part, right_part, "gy", block_ratio)
    left_sum = left_excl + ratio * lead_first * first
    right_sum = right_excl + ratio * tail_last * last

    row_pos = start + within
    left_gain = (couple * scaling) * one_minus(length - row_pos) * jnp.exp(within * log_decay)
    right_gain = (couple * scaling) * one_minus(row_pos + 1.0) * jnp.exp((y_rows - 1.0 - within) * log_decay)
    return solved + left_gain[:, None, None] * left_sum[None] + right_gain[:, None, None] * right_sum[None]


def explicit_full(values, line_dim, diffusion):
    width = [(0, 0)] * values.ndim
    width[line_dim] = (1, 1)
    padded = jnp.pad(values, width)
    length = values.shape[line_dim]
    before = lax.slice_in_dim(padded, 0, length, axis=line_dim)
    behind = lax.slice_in_dim(padded, 2, length + 2, axis=line_dim)
    return (1.0 - 2.4 * diffusion) * values + (0.1 + 1.2 * diffusion) * (before + behind)


def full_inverse(length, diffusion):
    pos = jnp.arange(length, dtype=jnp.float32)
    return green_table(pos[:, None], pos[None, :], length, diffusion)


def folded_inverse(length, diffusion):
    inverse = full_inverse(length, diffusion)
    shift_sum = jnp.eye(length, k=1, dtype=jnp.float32) + jnp.eye(length, k=-1, dtype=jnp.float32)
    explicit = (1.0 - 2.4 * diffusion) * jnp.eye(length, dtype=jnp.float32) + (0.1 + 1.2 * diffusion) * shift_sum
    return jnp.dot(inverse, explicit, precision=HIGHEST)


def x_solve(values, diffusion):
    combined = folded_inverse(values.shape[2], diffusion)
    return jnp.einsum("azj,ij->azi", values, combined, precision=HIGHEST)


def z_solve(values, diffusion):
    combined = folded_inverse(values.shape[1], diffusion)
    return jnp.einsum("ij,ajx->aix", combined, values, precision=HIGHEST)


CHUNKS = 2


def per_device(field):
    diffusion = float(LAMBDA)
    y_rows = field.shape[0]
    edges = jnp.stack([field[0], field[y_rows - 1]])
    edge_x = x_solve(edges, diffusion)
    along_x = x_solve(field, diffusion)
    along_y = y_solve(along_x, edge_x[0:1], edge_x[1:2], diffusion)
    width = along_y.shape[2] // CHUNKS
    parts = []
    for k in range(CHUNKS):
        piece = along_y[:, :, k * width:(k + 1) * width]
        pencils = lax.all_to_all(piece, "gz", split_axis=0, concat_axis=1, tiled=True)
        parts.append(z_solve(pencils, diffusion))
    return jnp.concatenate(parts, axis=2)


def solution(mesh):
    placed = (P("gy", "gz", None),)
    return jax.shard_map(
        per_device,
        mesh=mesh,
        in_specs=placed,
        out_specs=P(("gy", "gz"), None, None),
        check_vma=False,
    )
```

```python
import math

import jax
import jax.numpy as jnp
from jax import lax
from jax.sharding import PartitionSpec as P

BLK = 128
LAMBDA = 9216


HIGHEST = lax.Precision.HIGHEST


def padded_2(cells, sides, width):
    for axis, dim in sides:
        count = lax.axis_size(axis)
        ends = count - 1
        head = lax.slice_in_dim(cells, 0, width, axis=dim)
        tail = lax.slice_in_dim(cells, cells.shape[dim] - width, cells.shape[dim], axis=dim)
        cells = jnp.concatenate(
            [
                lax.ppermute(tail, axis, [(i, (i + 1) % count) for i in range(ends)]),
                cells,
                lax.ppermute(head, axis, [((i + 1) % count, i) for i in range(ends)]),
            ],
            axis=dim,
        )
    return cells


def decay_constants(diffusion, length):
    diagonal = 1.0 + 2.4 * diffusion
    off_diag = 0.1 - 1.2 * diffusion
    big_root = 0.5 * (diagonal + math.sqrt(diagonal * diagonal - 4.0 * off_diag * off_diag))
    decay_ratio = -off_diag / big_root
    log_decay = math.log(decay_ratio)
    scaling = 1.0 / (
        big_root
        * (1.0 - decay_ratio * decay_ratio)
        * (1.0 - math.exp(2.0 * log_decay * (length + 1)))
    )
    return (log_decay, scaling)


def green_table(row_pos, col_pos, length, diffusion):
    log_decay, scaling = decay_constants(diffusion, length)
    nearer = jnp.minimum(row_pos, col_pos)
    farther = jnp.maximum(row_pos, col_pos)
    return (
        scaling
        * jnp.exp((farther - nearer) * log_decay)
        * -jnp.expm1((nearer + 1.0) * (2.0 * log_decay))
        * -jnp.expm1((length - farther) * (2.0 * log_decay))
    )


def explicit_local(values, line_dim, diffusion):
    length = values.shape[line_dim]
    zeros_rim = jnp.zeros_like(lax.slice_in_dim(values, 0, 1, axis=line_dim))
    before = jnp.concatenate(
        [zeros_rim, lax.slice_in_dim(values, 0, length - 1, axis=line_dim)], axis=line_dim
    )
    behind = jnp.concatenate(
        [lax.slice_in_dim(values, 1, length, axis=line_dim), zeros_rim], axis=line_dim
    )
    return (1.0 - 2.4 * diffusion) * values + (0.1 + 1.2 * diffusion) * (before + behind)


def line_solve(values, line_dim, diffusion, block_len):
    length = values.shape[line_dim]
    pieces = length // block_len
    couple = 1.2 * diffusion - 0.1
    within = jnp.arange(block_len, dtype=jnp.float32)
    local_inverse = green_table(within[:, None], within[None, :], block_len, diffusion)
    piece_pos = jnp.arange(pieces, dtype=jnp.float32)
    side_pos = jnp.arange(2, dtype=jnp.float32)
    row_pos = piece_pos[:, None, None, None] * block_len + within[None, :, None, None]
    col_pos = (
        piece_pos[None, None, :, None] * block_len
        - 1.0
        + side_pos[None, None, None, :] * (block_len + 1.0)
    )
    coupling = couple * green_table(row_pos, col_pos, length, diffusion)
    if line_dim == 2:
        lead_len, tail_len = (values.shape[0], values.shape[1])
        splitted = values.reshape(lead_len, tail_len, pieces, block_len)
        solved = jnp.einsum("abqj,ij->abqi", splitted, local_inverse, precision=HIGHEST)
        rim_values = jnp.stack([solved[..., 0], solved[..., block_len - 1]], axis=-1)
        corrected = solved + jnp.einsum("abks,qiks->abqi", rim_values, coupling, precision=HIGHEST)
        return corrected.reshape(lead_len, tail_len, length)
    lead_len, tail_len = (values.shape[0], values.shape[2])
    splitted = values.reshape(lead_len, pieces, block_len, tail_len)
    solved = jnp.einsum("aqjb,ij->aqib", splitted, local_inverse, precision=HIGHEST)
    rim_values = jnp.stack([solved[:, :, 0, :], solved[:, :, block_len - 1, :]], axis=2)
    corrected = solved + jnp.einsum("aksb,qiks->aqib", rim_values, coupling, precision=HIGHEST)
    return corrected.reshape(lead_len, length, tail_len)


def shifted(values, axis, step):
    count = lax.axis_size(axis)
    if step > 0:
        pairs = [(i, i + step) for i in range(count - step)]
    else:
        pairs = [(i - step, i) for i in range(count + step)]
    return lax.ppermute(values, axis, pairs)


def butterfly_scans(left, right, axis, ratio):
    count = lax.axis_size(axis)
    assert count & (count - 1) == 0
    me = lax.axis_index(axis)
    left_total, right_total = left, right
    left_excl = jnp.zeros_like(left)
    right_excl = jnp.zeros_like(right)
    half = 1
    while half < count:
        pairs = [(i, i ^ half) for i in range(count)]
        got = lax.ppermute(jnp.stack([left_total, right_total]), axis, pairs)
        upper = (me & half) != 0
        base = me - (me % (2 * half))
        mid_gap = (me - base - half).astype(jnp.float32)
        low_gap = (base + half - 1 - me).astype(jnp.float32)
        left_gain = jnp.where(upper, jnp.exp(mid_gap * math.log(ratio)), 0.0)
        right_gain = jnp.where(upper, 0.0, jnp.exp(low_gap * math.log(ratio)))
        left_excl = left_excl + left_gain * got[0]
        right_excl = right_excl + right_gain * got[1]
        decay = ratio ** half
        left_total = jnp.where(upper, left_total + decay * got[0], decay * left_total + got[0])
        right_total = jnp.where(upper, got[1] + decay * right_total, right_total + decay * got[1])
        half *= 2
    return left_excl, right_excl


def y_solve(along_x, head, tail, diffusion):
    y_rows = along_x.shape[0]
    before = lax.ppermute(tail, "gy", [(i, i + 1) for i in range(lax.axis_size("gy") - 1)])
    behind = lax.ppermute(head, "gy", [(i + 1, i) for i in range(lax.axis_size("gy") - 1)])
    within = jnp.arange(y_rows, dtype=jnp.float32)
    local_inverse = green_table(within[:, None], within[None, :], y_rows, diffusion)
    side = 0.1 + 1.2 * diffusion
    shift_sum = jnp.eye(y_rows, k=1, dtype=jnp.float32) + jnp.eye(y_rows, k=-1, dtype=jnp.float32)
    explicit = (1.0 - 2.4 * diffusion) * jnp.eye(y_rows, dtype=jnp.float32) + side * shift_sum
    combined = jnp.dot(local_inverse, explicit, precision=HIGHEST)
    enter = side * local_inverse[:, 0]
    leave = side * local_inverse[:, y_rows - 1]

    def apply(rows, weights):
        picked = jnp.einsum("ij,jzx->izx", weights[rows], along_x, precision=HIGHEST)
        return picked + enter[rows][:, None, None] * before + leave[rows][:, None, None] * behind

    def rim(row):
        weighted = jnp.sum(combined[row][:, None, None] * along_x, axis=0)
        return weighted + enter[row] * before[0] + leave[row] * behind[0]

    rims = jnp.stack([rim(0), rim(y_rows - 1)])
    solved = lax.optimization_barrier(apply(jnp.arange(y_rows), combined))
    first, last = rims[0], rims[1]

    devices = lax.axis_size("gy")
    length = devices * y_rows
    log_decay, scaling = decay_constants(diffusion, length)
    ratio = math.exp(log_decay)
    block_ratio = math.exp(log_decay * y_rows)
    couple = 1.2 * diffusion - 0.1
    start = lax.axis_index("gy").astype(jnp.float32) * y_rows

    def one_minus(power):
        return -jnp.expm1(power * (2.0 * log_decay))

    lead_first = one_minus(start)
    tail_last = one_minus(length - start - y_rows)
    left_part = ratio ** (y_rows + 1) * lead_first * first + one_minus(start + y_rows + 1) * last
    right_part = one_minus(length - start + 1) * first + ratio ** (y_rows + 1) * tail_last * last
    left_excl, right_excl = butterfly_scans(left_part, right_part, "gy", block_ratio)
    left_sum = left_excl + ratio * lead_first * first
    right_sum = right_excl + ratio * tail_last * last

    row_pos = start + within
    left_gain = (couple * scaling) * one_minus(length - row_pos) * jnp.exp(within * log_decay)
    right_gain = (couple * scaling) * one_minus(row_pos + 1.0) * jnp.exp((y_rows - 1.0 - within) * log_decay)
    return solved + left_gain[:, None, None] * left_sum[None] + right_gain[:, None, None] * right_sum[None]


def explicit_full(values, line_dim, diffusion):
    width = [(0, 0)] * values.ndim
    width[line_dim] = (1, 1)
    padded = jnp.pad(values, width)
    length = values.shape[line_dim]
    before = lax.slice_in_dim(padded, 0, length, axis=line_dim)
    behind = lax.slice_in_dim(padded, 2, length + 2, axis=line_dim)
    return (1.0 - 2.4 * diffusion) * values + (0.1 + 1.2 * diffusion) * (before + behind)


def full_inverse(length, diffusion):
    pos = jnp.arange(length, dtype=jnp.float32)
    return green_table(pos[:, None], pos[None, :], length, diffusion)


def folded_inverse(length, diffusion):
    inverse = full_inverse(length, diffusion)
    shift_sum = jnp.eye(length, k=1, dtype=jnp.float32) + jnp.eye(length, k=-1, dtype=jnp.float32)
    explicit = (1.0 - 2.4 * diffusion) * jnp.eye(length, dtype=jnp.float32) + (0.1 + 1.2 * diffusion) * shift_sum
    return jnp.dot(inverse, explicit, precision=HIGHEST)


def x_solve(values, diffusion):
    combined = folded_inverse(values.shape[2], diffusion)
    return jnp.einsum("azj,ij->azi", values, combined, precision=HIGHEST)


def z_solve(values, diffusion):
    combined = folded_inverse(values.shape[1], diffusion)
    batched = jnp.broadcast_to(combined, (values.shape[0],) + combined.shape)
    return jnp.einsum("aij,ajx->aix", batched, values, precision=HIGHEST)


CHUNKS = 2


def per_device(field):
    diffusion = float(LAMBDA)
    y_rows = field.shape[0]
    edges = jnp.stack([field[0], field[y_rows - 1]])
    edge_x = x_solve(edges, diffusion)
    along_x = x_solve(field, diffusion)
    along_y = y_solve(along_x, edge_x[0:1], edge_x[1:2], diffusion)
    width = along_y.shape[2] // CHUNKS
    parts = []
    for k in range(CHUNKS):
        piece = along_y[:, :, k * width:(k + 1) * width]
        pencils = lax.all_to_all(piece, "gz", split_axis=0, concat_axis=1, tiled=True)
        parts.append(z_solve(pencils, diffusion))
    return jnp.concatenate(parts, axis=2)


def solution(mesh):
    placed = (P("gy", "gz", None),)
    return jax.shard_map(
        per_device,
        mesh=mesh,
        in_specs=placed,
        out_specs=P(("gy", "gz"), None, None),
        check_vma=False,
    )
```
